256 devices in a mesh: dp: 8 (over x_lo, y), fsdp: 32 (over z, x_hi, core).
Axes of the slice: x: 4 (x_hi: 2, x_lo: 2; x = x_hi * 2 + x_lo), y: 4, z: 8, core: 2. Of those that a mesh axis runs over, the one named last changes fastest.
Arguments:
- states: bfloat16 [6144, 1024], P('dp'), may hold values from -1200 to 1200
- w_in: bfloat16 [1024, 4096], P(None, 'fsdp'), may hold values from -0.1875 to 0.1875
- w_out: bfloat16 [4096, 1024], P('fsdp'), may hold values from -0.09375 to 0.09375
- precision: float32 [1024], replicated, may hold values from 0.125 to 1
- grad_in: float32 [1024, 4096], P(None, 'fsdp'), may hold values from -75 to 75
- grad_out: float32 [4096, 1024], P('fsdp'), may hold values from -75 to 75
Outputs:
- solution_in: float32 [1024, 4096], P(None, 'fsdp')
- solution_out: float32 [4096, 1024], P('fsdp')
- residual_in: float32 [1024, 4096], P(None, 'fsdp')
- residual_out: float32 [4096, 1024], P('fsdp')
The draws below stay inside these ranges and needn't reach their ends.
All inputs are finite; a program needn't handle non-finite values.
Results may differ from the reference program's by a relative error of at most 0.025.
Values may be sent and summed in bfloat16 or wider, within the bound.
No kernel may reach another device: no remote copies, remote signals or barrier semaphores. Data moves between devices by JAX's collectives and lax.ppermute only.
A program may use at most 64 MiB of HBM per device.

```python
import math
import jax
import jax.numpy as jnp
from jax import lax

D = 1024
H = 4096
ITERS = 3
STATES = 6144
N_FSDP = 32


def rising_scale(length, rise_base):
    position = jnp.arange(length, dtype=jnp.float32) / length
    return rise_base ** position


def rough_factor(key, row_total, col_total):
    return jnp.exp(jax.random.uniform(key, (row_total, col_total), jnp.float32, math.log(0.5), math.log(2.0)))


def draw_states(key, part):
    subkeys = jax.random.split(key, 3)
    base_field = jnp.clip(jax.random.normal(subkeys[0], (STATES, D), jnp.float32), -6.0, 6.0)
    top_log = math.log(10.0)
    row_scale = jnp.exp(jax.random.uniform(subkeys[1], (STATES, 1), jnp.float32, 0.0, top_log))
    col_scale = jnp.exp(jax.random.uniform(subkeys[2], (1, D), jnp.float32, 0.0, top_log))
    return (base_field * row_scale * col_scale).astype(jnp.bfloat16)


def draw_grad_in(key, part):
    subkeys = jax.random.split(key, 3)
    base_field = jnp.clip(jax.random.normal(subkeys[0], (D, H), jnp.float32), -6.0, 6.0)
    rise_scale = rising_scale(H, 3.0)
    return base_field * rough_factor(subkeys[2], D, H) * rise_scale[None, :]


def draw_grad_out(key, part):
    subkeys = jax.random.split(key, 3)
    base_field = jnp.clip(jax.random.normal(subkeys[0], (H, D), jnp.float32), -6.0, 6.0)
    rise_scale = rising_scale(H, 3.0)
    return base_field * rough_factor(subkeys[2], H, D) * rise_scale[:, None]


def level_of(stream_key, extent, cuts, least, largest):
    def one(dim, shards_of):
        heights = jax.random.uniform(jax.random.fold_in(jax.random.fold_in(stream_key, 6), dim), (shards_of,), jnp.float32, least / len(cuts), largest / len(cuts))
        return jnp.repeat(jnp.exp(heights), extent[dim] // shards_of).reshape((-1,) + (1,) * (len(extent) - dim - 1))

    loudness = one(*cuts[0])
    for cut in cuts[1:]:
        loudness = loudness * one(*cut)
    return loudness


def scatter_about(own_key, shape, deviation, bound, pieces=(), kind=jnp.bfloat16):
    array = deviation * jax.random.normal(own_key, shape, jnp.float32)
    if pieces:
        array = array * level_of(own_key, shape, pieces, -0.22, 0.18)
    return jnp.clip(array, -bound, bound).astype(kind)


def setup_inputs(seed: int = 0) -> dict:
    keys = jax.random.split(jax.random.key(seed), 7)
    states = draw_states(jax.random.fold_in(keys[6], 71), 0)
    w_in = scatter_about(keys[1], (D, H), D ** -0.5, 0.1875, ((1, 32),))
    w_out = scatter_about(keys[2], (H, D), H ** -0.5, 0.09375, ((0, 32),))
    precision = jnp.clip(jnp.exp(jax.random.uniform(keys[3], (D,), jnp.float32, math.log(0.125), math.log(1.0))), 0.125, 1.0)
    grad_in = draw_grad_in(jax.random.fold_in(keys[6], 71), 0)
    grad_out = draw_grad_out(jax.random.fold_in(keys[6], 71), 0)
    return dict(states=states, w_in=w_in, w_out=w_out, precision=precision, grad_in=grad_in, grad_out=grad_out)


damping = 0.2
norm_eps = 1e-05

def silu_slope(preact):
    gating = jax.nn.sigmoid(preact)
    return gating * (1.0 + preact * (1.0 - gating))

def fisher_product(direction_in, direction_out, normed, hidden_act, slope_act, w_out, metric):
    tangent_in = direction_in.astype(jnp.bfloat16)
    tangent_out = direction_out.astype(jnp.bfloat16)
    pre_tangent = jnp.dot(normed, tangent_in, preferred_element_type=jnp.float32)
    inner_tangent = (slope_act * pre_tangent).astype(jnp.bfloat16)
    block_width = H // N_FSDP

    def add_block(running, block_index):
        offset = (block_index * block_width).astype(jnp.int32)
        block_term = jnp.dot(lax.dynamic_slice_in_dim(inner_tangent, offset, block_width, 1), lax.dynamic_slice_in_dim(w_out, offset, block_width, 0), preferred_element_type=jnp.float32)
        block_term = block_term + jnp.dot(lax.dynamic_slice_in_dim(hidden_act, offset, block_width, 1), lax.dynamic_slice_in_dim(tangent_out, offset, block_width, 0), preferred_element_type=jnp.float32)
        rounded = lax.optimization_barrier(block_term.astype(jnp.bfloat16))
        return (running + rounded.astype(jnp.float32), None)
    out_tangent = lax.scan(add_block, jnp.zeros((STATES, D), jnp.float32), jnp.arange(N_FSDP, dtype=jnp.int32))[0]
    cotangent = (out_tangent * metric).astype(jnp.bfloat16)
    back_act = jnp.dot(cotangent, w_out.T, preferred_element_type=jnp.float32)
    grad_pre = (slope_act * back_act).astype(jnp.bfloat16)
    fisher_out = jnp.dot(hidden_act.T, cotangent, preferred_element_type=jnp.float32) + damping * direction_out
    fisher_in = jnp.dot(normed.T, grad_pre, preferred_element_type=jnp.float32) + damping * direction_in
    return (fisher_in, fisher_out)

def reference(states, w_in, w_out, precision, grad_in, grad_out):
    wide_states = states.astype(jnp.float32)
    mean_square = lax.optimization_barrier(jnp.mean(wide_states * wide_states, axis=1, keepdims=True))
    normed = (wide_states * lax.rsqrt(mean_square + norm_eps)).astype(jnp.bfloat16)
    preact = jnp.dot(normed, w_in, preferred_element_type=jnp.float32)
    hidden_act = jax.nn.silu(preact).astype(jnp.bfloat16)
    slope_act = silu_slope(preact)
    metric = precision / STATES
    solution_in = jnp.zeros_like(grad_in)
    solution_out = jnp.zeros_like(grad_out)
    residual_in, residual_out = (grad_in, grad_out)
    direction_in, direction_out = (grad_in, grad_out)
    norm_now = jnp.sum(residual_in * residual_in) + jnp.sum(residual_out * residual_out)
    for iteration in range(ITERS):
        fisher_in, fisher_out = fisher_product(direction_in, direction_out, normed, hidden_act, slope_act, w_out, metric)
        quadratic = jnp.sum(direction_in * fisher_in) + jnp.sum(direction_out * fisher_out)
        step_size = norm_now / quadratic
        solution_in = solution_in + step_size * direction_in
        solution_out = solution_out + step_size * direction_out
        residual_in = residual_in - step_size * fisher_in
        residual_out = residual_out - step_size * fisher_out
        norm_next = jnp.sum(residual_in * residual_in) + jnp.sum(residual_out * residual_out)
        direction_in = residual_in + norm_next / norm_now * direction_in
        direction_out = residual_out + norm_next / norm_now * direction_out
        norm_now = norm_next
    return (solution_in, solution_out, residual_in, residual_out)
```

```python
import jax
import jax.numpy as jnp
from jax import lax
from jax.sharding import PartitionSpec as P

ITERS = 3


damping = 0.2
norm_eps = 1e-05


def silu_slope(preact):
    gating = jax.nn.sigmoid(preact)
    return gating * (1.0 + preact * (1.0 - gating))


def contract_rows(left_side, right_side):
    return lax.dot_general(
        left_side, right_side, (((0,), (0,)), ((), ())), preferred_element_type=jnp.float32
    )


def local_dot(first_in, first_out, second_in, second_out):
    return jnp.sum(first_in * second_in) + jnp.sum(first_out * second_out)


def xor_pairs(size, bit):
    return [(i, i ^ bit) for i in range(size)]


def stages_of(size):
    count = size.bit_length() - 1
    assert 1 << count == size
    return count


def scalar_sum(values, axis):
    size = lax.axis_size(axis)
    gathered = lax.all_to_all(jnp.broadcast_to(values[None], (size,) + values.shape), axis, 0, 0)
    return jnp.sum(gathered, axis=0)


def doubling_sum(parts, axis):
    size = lax.axis_size(axis)
    for stage in range(stages_of(size)):
        pairs = xor_pairs(size, 1 << stage)
        parts = tuple(part + lax.ppermute(part, axis, pairs) for part in parts)
    return parts


def halving_reduce(term, axis):
    size = lax.axis_size(axis)
    index = lax.axis_index(axis)
    kept = term.astype(jnp.float32)
    for stage in range(stages_of(size)):
        half = kept.shape[0] // 2
        bit = (index >> stage) & 1
        send = lax.dynamic_slice_in_dim(kept, (1 - bit) * half, half, 0)
        keep = lax.dynamic_slice_in_dim(kept, bit * half, half, 0)
        got = lax.ppermute(send.astype(jnp.bfloat16), axis, xor_pairs(size, 1 << stage))
        kept = keep + got.astype(jnp.float32)
    return kept


def doubling_gather(chunk, axis):
    size = lax.axis_size(axis)
    index = lax.axis_index(axis)
    for stage in reversed(range(stages_of(size))):
        bit = (index >> stage) & 1
        other = lax.ppermute(chunk, axis, xor_pairs(size, 1 << stage))
        chunk = jnp.where(
            bit == 0, jnp.concatenate([chunk, other], 0), jnp.concatenate([other, chunk], 0)
        )
    return chunk


def fisher_product(direction_in, direction_out, normed, hidden_act, slope_act, w_out, metric):
    tangent_in = direction_in.astype(jnp.bfloat16)
    tangent_out = direction_out.astype(jnp.bfloat16)
    pre_tangent = jnp.dot(normed, tangent_in, preferred_element_type=jnp.float32)
    inner_tangent = (slope_act * pre_tangent).astype(jnp.bfloat16)
    partial_out = jnp.dot(inner_tangent, w_out, preferred_element_type=jnp.float32)
    partial_out = partial_out + jnp.dot(hidden_act, tangent_out, preferred_element_type=jnp.float32)
    out_chunk = halving_reduce(partial_out.astype(jnp.bfloat16), "fsdp")
    cotangent = doubling_gather((out_chunk * metric).astype(jnp.bfloat16), "fsdp")
    back_act = lax.dot_general(
        cotangent, w_out, (((1,), (1,)), ((), ())), preferred_element_type=jnp.float32
    )
    grad_pre = (slope_act * back_act).astype(jnp.bfloat16)
    part_out = contract_rows(hidden_act, cotangent)
    part_in = contract_rows(normed, grad_pre)
    fisher_in, fisher_out = doubling_sum((part_in, part_out), "dp")
    fisher_in = fisher_in + damping * direction_in
    fisher_out = fisher_out + damping * direction_out
    quadratic = scalar_sum(local_dot(direction_in, direction_out, fisher_in, fisher_out)[None], "fsdp")[0]
    return (fisher_in, fisher_out, quadratic)


def global_norm(vector_in, vector_out):
    return scalar_sum(local_dot(vector_in, vector_out, vector_in, vector_out)[None], "fsdp")[0]


def on_device(states, w_in, w_out, precision, grad_in, grad_out):
    row_count = states.shape[0]
    metric = precision / (row_count * lax.axis_size("dp"))
    wide_states = states.astype(jnp.float32)
    mean_square = jnp.mean(wide_states * wide_states, axis=1, keepdims=True)
    normed = (wide_states * lax.rsqrt(mean_square + norm_eps)).astype(jnp.bfloat16)
    preact = jnp.dot(normed, w_in, preferred_element_type=jnp.float32)
    hidden_act = jax.nn.silu(preact).astype(jnp.bfloat16)
    slope_act = silu_slope(preact)
    solution_in = jnp.zeros_like(grad_in)
    solution_out = jnp.zeros_like(grad_out)
    residual_in, residual_out = (grad_in, grad_out)
    direction_in, direction_out = (grad_in, grad_out)
    norm_now = global_norm(residual_in, residual_out)
    for iteration in range(ITERS):
        fisher_in, fisher_out, quadratic = fisher_product(
            direction_in, direction_out, normed, hidden_act, slope_act, w_out, metric
        )
        step_size = norm_now / quadratic
        solution_in = solution_in + step_size * direction_in
        solution_out = solution_out + step_size * direction_out
        residual_in = residual_in - step_size * fisher_in
        residual_out = residual_out - step_size * fisher_out
        if iteration + 1 < ITERS:
            norm_next = global_norm(residual_in, residual_out)
            direction_in = residual_in + norm_next / norm_now * direction_in
            direction_out = residual_out + norm_next / norm_now * direction_out
            norm_now = norm_next
    return (solution_in, solution_out, residual_in, residual_out)


def solution(mesh):
    return jax.shard_map(
        on_device,
        mesh=mesh,
        in_specs=(
            P("dp", None),
            P(None, "fsdp"),
            P("fsdp", None),
            P(),
            P(None, "fsdp"),
            P("fsdp", None),
        ),
        out_specs=(P(None, "fsdp"), P("fsdp", None), P(None, "fsdp"), P("fsdp", None)),
        check_vma=False,
    )
```

```python
import jax
import jax.numpy as jnp
from jax import lax
from jax.sharding import PartitionSpec as P

ITERS = 3


damping = 0.2
norm_eps = 1e-05


def silu_slope(preact):
    gating = jax.nn.sigmoid(preact)
    return gating * (1.0 + preact * (1.0 - gating))


def contract_rows(left_side, right_side):
    return lax.dot_general(
        left_side, right_side, (((0,), (0,)), ((), ())), preferred_element_type=jnp.float32
    )


def xor_pairs(size, bit):
    return [(i, i ^ bit) for i in range(size)]


def stages_of(size):
    count = size.bit_length() - 1
    assert 1 << count == size
    return count


def scalar_sum(values, axis):
    size = lax.axis_size(axis)
    gathered = lax.all_to_all(jnp.broadcast_to(values[None], (size,) + values.shape), axis, 0, 0)
    return jnp.sum(gathered, axis=0)


def doubling_sum(parts, axis):
    size = lax.axis_size(axis)
    for stage in range(stages_of(size)):
        pairs = xor_pairs(size, 1 << stage)
        parts = tuple(part + lax.ppermute(part, axis, pairs) for part in parts)
    return parts


def halving_reduce(term, axis):
    size = lax.axis_size(axis)
    index = lax.axis_index(axis)
    kept = term.astype(jnp.float32)
    for stage in range(stages_of(size)):
        half = kept.shape[0] // 2
        bit = (index >> stage) & 1
        send = lax.dynamic_slice_in_dim(kept, (1 - bit) * half, half, 0)
        keep = lax.dynamic_slice_in_dim(kept, bit * half, half, 0)
        got = lax.ppermute(send.astype(jnp.bfloat16), axis, xor_pairs(size, 1 << stage))
        kept = keep + got.astype(jnp.float32)
    return kept


def doubling_gather(chunk, axis):
    size = lax.axis_size(axis)
    index = lax.axis_index(axis)
    for stage in reversed(range(stages_of(size))):
        bit = (index >> stage) & 1
        other = lax.ppermute(chunk, axis, xor_pairs(size, 1 << stage))
        chunk = jnp.where(
            bit == 0, jnp.concatenate([chunk, other], 0), jnp.concatenate([other, chunk], 0)
        )
    return chunk


def fisher_product(direction, normed, hidden_act, slope_act, w_out, metric, width):
    tangent = direction.astype(jnp.bfloat16)
    tangent_in = tangent[:, :width]
    tangent_out_t = tangent[:, width:]
    pre_tangent = jnp.dot(normed, tangent_in, preferred_element_type=jnp.float32)
    inner_tangent = (slope_act * pre_tangent).astype(jnp.bfloat16)
    partial_out = jnp.dot(inner_tangent, w_out, preferred_element_type=jnp.float32)
    partial_out = partial_out + lax.dot_general(
        hidden_act, tangent_out_t, (((1,), (1,)), ((), ())), preferred_element_type=jnp.float32
    )
    out_chunk = halving_reduce(partial_out.astype(jnp.bfloat16), "fsdp")
    cotangent = doubling_gather((out_chunk * metric).astype(jnp.bfloat16), "fsdp")
    back_act = lax.dot_general(
        cotangent, w_out, (((1,), (1,)), ((), ())), preferred_element_type=jnp.float32
    )
    grad_pre = (slope_act * back_act).astype(jnp.bfloat16)
    part_out_t = contract_rows(cotangent, hidden_act)
    part_in = contract_rows(normed, grad_pre)
    (fisher,) = doubling_sum((jnp.concatenate([part_in, part_out_t], axis=1),), "dp")
    return fisher + damping * direction


def on_device(states, w_in, w_out, precision, grad_in, grad_out):
    row_count = states.shape[0]
    width = w_in.shape[1]
    metric = precision / (row_count * lax.axis_size("dp"))
    wide_states = states.astype(jnp.float32)
    mean_square = jnp.mean(wide_states * wide_states, axis=1, keepdims=True)
    normed = (wide_states * lax.rsqrt(mean_square + norm_eps)).astype(jnp.bfloat16)
    preact = jnp.dot(normed, w_in, preferred_element_type=jnp.float32)
    hidden_act = jax.nn.silu(preact).astype(jnp.bfloat16)
    slope_act = silu_slope(preact)
    residual = jnp.concatenate([grad_in, grad_out.T], axis=1)
    solution_now = jnp.zeros_like(residual)
    direction = residual
    norm_now = scalar_sum(jnp.sum(residual * residual)[None], "fsdp")[0]
    for iteration in range(ITERS):
        fisher = fisher_product(direction, normed, hidden_act, slope_act, w_out, metric, width)
        sums = jnp.stack(
            [jnp.sum(direction * fisher), jnp.sum(residual * fisher), jnp.sum(fisher * fisher)]
        )
        quadratic, cross, fisher_square = scalar_sum(sums, "fsdp")
        step_size = norm_now / quadratic
        solution_now = solution_now + step_size * direction
        residual = residual - step_size * fisher
        if iteration + 1 < ITERS:
            norm_next = norm_now - 2.0 * step_size * cross + step_size * step_size * fisher_square
            direction = residual + norm_next / norm_now * direction
            norm_now = norm_next
    return (
        solution_now[:, :width],
        solution_now[:, width:].T,
        residual[:, :width],
        residual[:, width:].T,
    )


def solution(mesh):
    return jax.shard_map(
        on_device,
        mesh=mesh,
        in_specs=(
            P("dp", None),
            P(None, "fsdp"),
            P("fsdp", None),
            P(),
            P(None, "fsdp"),
            P("fsdp", None),
        ),
        out_specs=(P(None, "fsdp"), P("fsdp", None), P(None, "fsdp"), P("fsdp", None)),
        check_vma=False,
    )
```

```python
import jax
import jax.numpy as jnp
from jax import lax
from jax.sharding import PartitionSpec as P

ITERS = 3


damping = 0.2
norm_eps = 1e-05


def silu_slope(preact):
    gating = jax.nn.sigmoid(preact)
    return gating * (1.0 + preact * (1.0 - gating))


def contract_rows(left_side, right_side):
    return lax.dot_general(
        left_side, right_side, (((0,), (0,)), ((), ())), preferred_element_type=jnp.float32
    )


def xor_pairs(size, bit):
    return [(i, i ^ bit) for i in range(size)]


def stages_of(size):
    count = size.bit_length() - 1
    assert 1 << count == size
    return count


def scalar_sum(values, axis):
    size = lax.axis_size(axis)
    gathered = lax.all_to_all(jnp.broadcast_to(values[None], (size,) + values.shape), axis, 0, 0)
    return jnp.sum(gathered, axis=0)


def doubling_sum(whole, axis, pieces=4):
    size = lax.axis_size(axis)
    count = stages_of(size)
    parts = jnp.split(whole, pieces, axis=0)
    for stage in range(count):
        parts = [
            part + lax.ppermute(part, axis, xor_pairs(size, 1 << ((stage + number) % count)))
            for number, part in enumerate(parts)
        ]
    return jnp.concatenate(parts, axis=0)


def split_permute(value, axis, pairs):
    if value.shape[0] < 192:
        return lax.ppermute(value, axis, pairs)
    upper, lower = jnp.split(value, 2, axis=0)
    return jnp.concatenate([lax.ppermute(upper, axis, pairs), lax.ppermute(lower, axis, pairs)], 0)


def halving_reduce(term, axis):
    size = lax.axis_size(axis)
    index = lax.axis_index(axis)
    kept = term.astype(jnp.float32)
    for stage in range(stages_of(size)):
        half = kept.shape[0] // 2
        bit = (index >> stage) & 1
        send = lax.dynamic_slice_in_dim(kept, (1 - bit) * half, half, 0)
        keep = lax.dynamic_slice_in_dim(kept, bit * half, half, 0)
        got = split_permute(send.astype(jnp.bfloat16), axis, xor_pairs(size, 1 << stage))
        kept = keep + got.astype(jnp.float32)
    return kept


def doubling_gather(chunk, axis):
    size = lax.axis_size(axis)
    index = lax.axis_index(axis)
    for stage in reversed(range(stages_of(size))):
        bit = (index >> stage) & 1
        other = split_permute(chunk, axis, xor_pairs(size, 1 << stage))
        chunk = jnp.where(
            bit == 0, jnp.concatenate([chunk, other], 0), jnp.concatenate([other, chunk], 0)
        )
    return chunk


def fisher_product(direction, normed, hidden_act, slope_act, w_out, metric, width):
    tangent = direction.astype(jnp.bfloat16)
    tangent_in = tangent[:, :width]
    tangent_out_t = tangent[:, width:]
    pre_tangent = jnp.dot(normed, tangent_in, preferred_element_type=jnp.float32)
    inner_tangent = (slope_act * pre_tangent).astype(jnp.bfloat16)
    partial_out = jnp.dot(inner_tangent, w_out, preferred_element_type=jnp.float32)
    partial_out = partial_out + lax.dot_general(
        hidden_act, tangent_out_t, (((1,), (1,)), ((), ())), preferred_element_type=jnp.float32
    )
    out_chunk = halving_reduce(partial_out.astype(jnp.bfloat16), "fsdp")
    cotangent = doubling_gather((out_chunk * metric).astype(jnp.bfloat16), "fsdp")
    back_act = lax.dot_general(
        cotangent, w_out, (((1,), (1,)), ((), ())), preferred_element_type=jnp.float32
    )
    grad_pre = (slope_act * back_act).astype(jnp.bfloat16)
    part_out_t = contract_rows(cotangent, hidden_act)
    part_in = contract_rows(normed, grad_pre)
    fisher = doubling_sum(jnp.concatenate([part_in, part_out_t], axis=1), "dp")
    return fisher + damping * direction


def on_device(states, w_in, w_out, precision, grad_in, grad_out):
    row_count = states.shape[0]
    width = w_in.shape[1]
    metric = precision / (row_count * lax.axis_size("dp"))
    wide_states = states.astype(jnp.float32)
    mean_square = jnp.mean(wide_states * wide_states, axis=1, keepdims=True)
    normed = (wide_states * lax.rsqrt(mean_square + norm_eps)).astype(jnp.bfloat16)
    preact = jnp.dot(normed, w_in, preferred_element_type=jnp.float32)
    hidden_act = jax.nn.silu(preact).astype(jnp.bfloat16)
    slope_act = silu_slope(preact)
    residual = jnp.concatenate([grad_in, grad_out.T], axis=1)
    solution_now = jnp.zeros_like(residual)
    direction = residual
    norm_now = scalar_sum(jnp.sum(residual * residual)[None], "fsdp")[0]
    for iteration in range(ITERS):
        fisher = fisher_product(direction, normed, hidden_act, slope_act, w_out, metric, width)
        sums = jnp.stack(
            [jnp.sum(direction * fisher), jnp.sum(residual * fisher), jnp.sum(fisher * fisher)]
        )
        quadratic, cross, fisher_square = scalar_sum(sums, "fsdp")
        step_size = norm_now / quadratic
        solution_now = solution_now + step_size * direction
        residual = residual - step_size * fisher
        if iteration + 1 < ITERS:
            norm_next = norm_now - 2.0 * step_size * cross + step_size * step_size * fisher_square
            direction = residual + norm_next / norm_now * direction
            norm_now = norm_next
    return (
        solution_now[:, :width],
        solution_now[:, width:].T,
        residual[:, :width],
        residual[:, width:].T,
    )


def solution(mesh):
    return jax.shard_map(
        on_device,
        mesh=mesh,
        in_specs=(
            P("dp", None),
            P(None, "fsdp"),
            P("fsdp", None),
            P(),
            P(None, "fsdp"),
            P("fsdp", None),
        ),
        out_specs=(P(None, "fsdp"), P("fsdp", None), P(None, "fsdp"), P("fsdp", None)),
        check_vma=False,
    )
```

```python
import jax
import jax.numpy as jnp
from jax import lax
from jax.sharding import PartitionSpec as P

ITERS = 3


damping = 0.2
norm_eps = 1e-05


def silu_slope(preact):
    gating = jax.nn.sigmoid(preact)
    return gating * (1.0 + preact * (1.0 - gating))


def contract_rows(left_side, right_side):
    return lax.dot_general(
        left_side, right_side, (((0,), (0,)), ((), ())), preferred_element_type=jnp.float32
    )


def xor_pairs(size, bit):
    return [(i, i ^ bit) for i in range(size)]


def stages_of(size):
    count = size.bit_length() - 1
    assert 1 << count == size
    return count


def scalar_sum(values, axis):
    size = lax.axis_size(axis)
    gathered = lax.all_to_all(jnp.broadcast_to(values[None], (size,) + values.shape), axis, 0, 0)
    return jnp.sum(gathered, axis=0)


def digit_groups(size, first_bits):
    count = stages_of(size)
    groups = [(0, min(first_bits, count))]
    if count > first_bits:
        groups.append((first_bits, count - first_bits))
    return groups


def spread_reduce(value, axis, groups, send_type):
    size = lax.axis_size(axis)
    index = lax.axis_index(axis)
    kept = value.astype(jnp.float32)
    for low, bits in groups:
        width = 1 << bits
        digit = (index >> low) & (width - 1)
        rows = kept.shape[0] // width
        total = lax.dynamic_slice_in_dim(kept, digit * rows, rows, 0)
        for offset in range(1, width):
            send = lax.dynamic_slice_in_dim(kept, (digit ^ offset) * rows, rows, 0)
            got = lax.ppermute(send.astype(send_type), axis, xor_pairs(size, offset << low))
            total = total + got.astype(jnp.float32)
        kept = total
    return kept


def spread_gather(chunk, axis, groups):
    size = lax.axis_size(axis)
    index = lax.axis_index(axis)
    for low, bits in reversed(groups):
        width = 1 << bits
        digit = (index >> low) & (width - 1)
        rows = chunk.shape[0]
        whole = jnp.zeros((rows * width,) + chunk.shape[1:], chunk.dtype)
        whole = lax.dynamic_update_slice_in_dim(whole, chunk, digit * rows, 0)
        for offset in range(1, width):
            got = lax.ppermute(chunk, axis, xor_pairs(size, offset << low))
            whole = lax.dynamic_update_slice_in_dim(whole, got, (digit ^ offset) * rows, 0)
        chunk = whole
    return chunk


def fisher_product(direction, normed, hidden_act, slope_act, w_out, metric, width):
    tangent = direction.astype(jnp.bfloat16)
    tangent_in = tangent[:, :width]
    tangent_out_t = tangent[:, width:]
    pre_tangent = jnp.dot(normed, tangent_in, preferred_element_type=jnp.float32)
    inner_tangent = (slope_act * pre_tangent).astype(jnp.bfloat16)
    partial_out = jnp.dot(inner_tangent, w_out, preferred_element_type=jnp.float32)
    partial_out = partial_out + lax.dot_general(
        hidden_act, tangent_out_t, (((1,), (1,)), ((), ())), preferred_element_type=jnp.float32
    )
    fsdp_groups = digit_groups(lax.axis_size("fsdp"), 2)
    out_chunk = spread_reduce(partial_out.astype(jnp.bfloat16), "fsdp", fsdp_groups, jnp.bfloat16)
    cotangent = spread_gather((out_chunk * metric).astype(jnp.bfloat16), "fsdp", fsdp_groups)
    back_act = lax.dot_general(
        cotangent, w_out, (((1,), (1,)), ((), ())), preferred_element_type=jnp.float32
    )
    grad_pre = (slope_act * back_act).astype(jnp.bfloat16)
    part_out_t = contract_rows(cotangent, hidden_act)
    part_in = contract_rows(normed, grad_pre)
    dp_groups = digit_groups(lax.axis_size("dp"), 3)
    fisher_chunk = spread_reduce(jnp.concatenate([part_in, part_out_t], axis=1), "dp", dp_groups, jnp.float32)
    fisher = spread_gather(fisher_chunk, "dp", dp_groups)
    return fisher + damping * direction


def on_device(states, w_in, w_out, precision, grad_in, grad_out):
    row_count = states.shape[0]
    width = w_in.shape[1]
    metric = precision / (row_count * lax.axis_size("dp"))
    wide_states = states.astype(jnp.float32)
    mean_square = jnp.mean(wide_states * wide_states, axis=1, keepdims=True)
    normed = (wide_states * lax.rsqrt(mean_square + norm_eps)).astype(jnp.bfloat16)
    preact = jnp.dot(normed, w_in, preferred_element_type=jnp.float32)
    hidden_act = jax.nn.silu(preact).astype(jnp.bfloat16)
    slope_act = silu_slope(preact)
    residual = jnp.concatenate([grad_in, grad_out.T], axis=1)
    solution_now = jnp.zeros_like(residual)
    direction = residual
    norm_now = scalar_sum(jnp.sum(residual * residual)[None], "fsdp")[0]
    for iteration in range(ITERS):
        fisher = fisher_product(direction, normed, hidden_act, slope_act, w_out, metric, width)
        sums = jnp.stack(
            [jnp.sum(direction * fisher), jnp.sum(residual * fisher), jnp.sum(fisher * fisher)]
        )
        quadratic, cross, fisher_square = scalar_sum(sums, "fsdp")
        step_size = norm_now / quadratic
        solution_now = solution_now + step_size * direction
        residual = residual - step_size * fisher
        if iteration + 1 < ITERS:
            norm_next = norm_now - 2.0 * step_size * cross + step_size * step_size * fisher_square
            direction = residual + norm_next / norm_now * direction
            norm_now = norm_next
    return (
        solution_now[:, :width],
        solution_now[:, width:].T,
        residual[:, :width],
        residual[:, width:].T,
    )


def solution(mesh):
    return jax.shard_map(
        on_device,
        mesh=mesh,
        in_specs=(
            P("dp", None),
            P(None, "fsdp"),
            P("fsdp", None),
            P(),
            P(None, "fsdp"),
            P("fsdp", None),
        ),
        out_specs=(P(None, "fsdp"), P("fsdp", None), P(None, "fsdp"), P("fsdp", None)),
        check_vma=False,
    )
```

```python
import jax
import jax.numpy as jnp
from jax import lax
from jax.sharding import PartitionSpec as P

ITERS = 3


damping = 0.2
norm_eps = 1e-05


def silu_slope(preact):
    gating = jax.nn.sigmoid(preact)
    return gating * (1.0 + preact * (1.0 - gating))


def contract_rows(left_side, right_side):
    return lax.dot_general(
        left_side, right_side, (((0,), (0,)), ((), ())), preferred_element_type=jnp.float32
    )


def xor_pairs(size, bit):
    return [(i, i ^ bit) for i in range(size)]


def stages_of(size):
    count = size.bit_length() - 1
    assert 1 << count == size
    return count


def scalar_sum(values, axis):
    size = lax.axis_size(axis)
    gathered = lax.all_to_all(jnp.broadcast_to(values[None], (size,) + values.shape), axis, 0, 0)
    return jnp.sum(gathered, axis=0)


def digit_groups(size, first_bits):
    count = stages_of(size)
    groups = [(0, min(first_bits, count))]
    if count > first_bits:
        groups.append((first_bits, count - first_bits))
    return groups


def spread_reduce(value, axis, groups, send_type):
    size = lax.axis_size(axis)
    index = lax.axis_index(axis)
    kept = value.astype(jnp.float32)
    for low, bits in groups:
        width = 1 << bits
        digit = (index >> low) & (width - 1)
        rows = kept.shape[0] // width
        total = lax.dynamic_slice_in_dim(kept, digit * rows, rows, 0)
        for offset in range(1, width):
            send = lax.dynamic_slice_in_dim(kept, (digit ^ offset) * rows, rows, 0)
            got = lax.ppermute(send.astype(send_type), axis, xor_pairs(size, offset << low))
            total = total + got.astype(jnp.float32)
        kept = total
    return kept


def spread_gather(chunk, axis, groups):
    size = lax.axis_size(axis)
    index = lax.axis_index(axis)
    for low, bits in reversed(groups):
        width = 1 << bits
        digit = (index >> low) & (width - 1)
        rows = chunk.shape[0]
        whole = jnp.zeros((rows * width,) + chunk.shape[1:], chunk.dtype)
        whole = lax.dynamic_update_slice_in_dim(whole, chunk, digit * rows, 0)
        for offset in range(1, width):
            got = lax.ppermute(chunk, axis, xor_pairs(size, offset << low))
            whole = lax.dynamic_update_slice_in_dim(whole, got, (digit ^ offset) * rows, 0)
        chunk = whole
    return chunk


def fisher_product(direction, normed, hidden_act, slope_act, w_out, metric, width):
    tangent = direction.astype(jnp.bfloat16)
    tangent_in = tangent[:, :width]
    tangent_out_t = tangent[:, width:]
    pre_tangent = jnp.dot(normed, tangent_in, preferred_element_type=jnp.float32)
    inner_tangent = (slope_act * pre_tangent).astype(jnp.bfloat16)
    partial_out = jnp.dot(inner_tangent, w_out, preferred_element_type=jnp.float32)
    partial_out = partial_out + lax.dot_general(
        hidden_act, tangent_out_t, (((1,), (1,)), ((), ())), preferred_element_type=jnp.float32
    )
    fsdp_groups = digit_groups(lax.axis_size("fsdp"), 2)
    out_chunk = spread_reduce(partial_out.astype(jnp.bfloat16), "fsdp", fsdp_groups, jnp.bfloat16)
    cotangent = spread_gather((out_chunk * metric).astype(jnp.bfloat16), "fsdp", fsdp_groups)
    back_act = lax.dot_general(
        cotangent, w_out, (((1,), (1,)), ((), ())), preferred_element_type=jnp.float32
    )
    grad_pre = (slope_act * back_act).astype(jnp.bfloat16)
    part_out_t = contract_rows(cotangent, hidden_act)
    part_in = contract_rows(normed, grad_pre)
    dp_groups = digit_groups(lax.axis_size("dp"), 3)
    fisher_chunk = spread_reduce(jnp.concatenate([part_in, part_out_t], axis=1), "dp", dp_groups, jnp.float32)
    fisher = spread_gather(fisher_chunk, "dp", dp_groups)
    return fisher + damping * direction


def on_device(states, w_in, w_out, precision, grad_in, grad_out):
    row_count = states.shape[0]
    width = w_in.shape[1]
    metric = precision / (row_count * lax.axis_size("dp"))
    wide_states = states.astype(jnp.float32)
    mean_square = jnp.mean(wide_states * wide_states, axis=1, keepdims=True)
    normed = (wide_states * lax.rsqrt(mean_square + norm_eps)).astype(jnp.bfloat16)
    preact = jnp.dot(normed, w_in, preferred_element_type=jnp.float32)
    hidden_act = jax.nn.silu(preact).astype(jnp.bfloat16)
    slope_act = silu_slope(preact)
    residual = jnp.concatenate([grad_in, grad_out.T], axis=1)

    def iterate(_, carry):
        solution_now, residual, direction = carry
        fisher = fisher_product(direction, normed, hidden_act, slope_act, w_out, metric, width)
        sums = jnp.stack(
            [
                jnp.sum(direction * fisher),
                jnp.sum(residual * fisher),
                jnp.sum(fisher * fisher),
                jnp.sum(residual * residual),
            ]
        )
        quadratic, cross, fisher_square, norm_now = scalar_sum(sums, "fsdp")
        step_size = norm_now / quadratic
        solution_now = solution_now + step_size * direction
        residual_next = residual - step_size * fisher
        norm_next = norm_now - 2.0 * step_size * cross + step_size * step_size * fisher_square
        direction = residual_next + norm_next / norm_now * direction
        return (solution_now, residual_next, direction)

    solution_now, residual, _ = lax.fori_loop(
        0, ITERS, iterate, (jnp.zeros_like(residual), residual, residual)
    )
    return (
        solution_now[:, :width],
        solution_now[:, width:].T,
        residual[:, :width],
        residual[:, width:].T,
    )


def solution(mesh):
    return jax.shard_map(
        on_device,
        mesh=mesh,
        in_specs=(
            P("dp", None),
            P(None, "fsdp"),
            P("fsdp", None),
            P(),
            P(None, "fsdp"),
            P("fsdp", None),
        ),
        out_specs=(P(None, "fsdp"), P("fsdp", None), P(None, "fsdp"), P("fsdp", None)),
        check_vma=False,
    )
```

```python
import jax
import jax.numpy as jnp
from jax import lax
from jax.sharding import PartitionSpec as P

ITERS = 3


damping = 0.2
norm_eps = 1e-05


def silu_slope(preact):
    gating = jax.nn.sigmoid(preact)
    return gating * (1.0 + preact * (1.0 - gating))


def contract_rows(left_side, right_side):
    return lax.dot_general(
        left_side, right_side, (((0,), (0,)), ((), ())), preferred_element_type=jnp.float32
    )


def xor_pairs(size, bit):
    return [(i, i ^ bit) for i in range(size)]


def stages_of(size):
    count = size.bit_length() - 1
    assert 1 << count == size
    return count


def scalar_sum(values, axis):
    names = axis if isinstance(axis, tuple) else (axis,)
    size = 1
    for name in names:
        size *= lax.axis_size(name)
    gathered = lax.all_to_all(jnp.broadcast_to(values[None], (size,) + values.shape), axis, 0, 0)
    return jnp.sum(gathered, axis=0)


def digit_groups(size, first_bits):
    count = stages_of(size)
    groups = [(0, min(first_bits, count))]
    if count > first_bits:
        groups.append((first_bits, count - first_bits))
    return groups


def spread_reduce(value, axis, groups, send_type):
    size = lax.axis_size(axis)
    index = lax.axis_index(axis)
    kept = value.astype(jnp.float32)
    for low, bits in groups:
        width = 1 << bits
        digit = (index >> low) & (width - 1)
        rows = kept.shape[0] // width
        total = lax.dynamic_slice_in_dim(kept, digit * rows, rows, 0)
        for offset in range(1, width):
            send = lax.dynamic_slice_in_dim(kept, (digit ^ offset) * rows, rows, 0)
            got = lax.ppermute(send.astype(send_type), axis, xor_pairs(size, offset << low))
            total = total + got.astype(jnp.float32)
        kept = total
    return kept


def spread_gather(chunk, axis, groups):
    size = lax.axis_size(axis)
    index = lax.axis_index(axis)
    for low, bits in reversed(groups):
        width = 1 << bits
        digit = (index >> low) & (width - 1)
        rows = chunk.shape[0]
        whole = jnp.zeros((rows * width,) + chunk.shape[1:], chunk.dtype)
        whole = lax.dynamic_update_slice_in_dim(whole, chunk, digit * rows, 0)
        for offset in range(1, width):
            got = lax.ppermute(chunk, axis, xor_pairs(size, offset << low))
            whole = lax.dynamic_update_slice_in_dim(whole, got, (digit ^ offset) * rows, 0)
        chunk = whole
    return chunk


def fisher_product(direction, residual, normed, hidden_act, slope_act, w_out, metric, width):
    tangent = direction.astype(jnp.bfloat16)
    tangent_in = tangent[:, :width]
    tangent_out_t = tangent[:, width:]
    pre_tangent = jnp.dot(normed, tangent_in, preferred_element_type=jnp.float32)
    inner_tangent = (slope_act * pre_tangent).astype(jnp.bfloat16)
    partial_out = jnp.dot(inner_tangent, w_out, preferred_element_type=jnp.float32)
    partial_out = partial_out + lax.dot_general(
        hidden_act, tangent_out_t, (((1,), (1,)), ((), ())), preferred_element_type=jnp.float32
    )
    fsdp_groups = digit_groups(lax.axis_size("fsdp"), 2)
    out_chunk = spread_reduce(partial_out.astype(jnp.bfloat16), "fsdp", fsdp_groups, jnp.bfloat16)
    cotangent = spread_gather((out_chunk * metric).astype(jnp.bfloat16), "fsdp", fsdp_groups)
    back_act = lax.dot_general(
        cotangent, w_out, (((1,), (1,)), ((), ())), preferred_element_type=jnp.float32
    )
    grad_pre = (slope_act * back_act).astype(jnp.bfloat16)
    part_out_t = contract_rows(cotangent, hidden_act)
    part_in = contract_rows(normed, grad_pre)
    dp_groups = digit_groups(lax.axis_size("dp"), 3)
    reduced = spread_reduce(jnp.concatenate([part_in, part_out_t], axis=1), "dp", dp_groups, jnp.float32)
    rows = reduced.shape[0]
    start = lax.axis_index("dp") * rows
    direction_chunk = lax.dynamic_slice_in_dim(direction, start, rows, 0)
    residual_chunk = lax.dynamic_slice_in_dim(residual, start, rows, 0)
    fisher_chunk = reduced + damping * direction_chunk
    sums = jnp.stack(
        [
            jnp.sum(direction_chunk * fisher_chunk),
            jnp.sum(residual_chunk * fisher_chunk),
            jnp.sum(fisher_chunk * fisher_chunk),
            jnp.sum(residual_chunk * residual_chunk),
        ]
    )
    fisher = spread_gather(fisher_chunk, "dp", dp_groups)
    return fisher, scalar_sum(sums, ("dp", "fsdp"))


def on_device(states, w_in, w_out, precision, grad_in, grad_out):
    row_count = states.shape[0]
    width = w_in.shape[1]
    metric = precision / (row_count * lax.axis_size("dp"))
    wide_states = states.astype(jnp.float32)
    mean_square = jnp.mean(wide_states * wide_states, axis=1, keepdims=True)
    normed = (wide_states * lax.rsqrt(mean_square + norm_eps)).astype(jnp.bfloat16)
    preact = jnp.dot(normed, w_in, preferred_element_type=jnp.float32)
    hidden_act = jax.nn.silu(preact).astype(jnp.bfloat16)
    slope_act = silu_slope(preact)
    residual = jnp.concatenate([grad_in, grad_out.T], axis=1)

    def iterate(_, carry):
        solution_now, residual, direction = carry
        fisher, sums = fisher_product(
            direction, residual, normed, hidden_act, slope_act, w_out, metric, width
        )
        quadratic, cross, fisher_square, norm_now = sums
        step_size = norm_now / quadratic
        solution_now = solution_now + step_size * direction
        residual_next = residual - step_size * fisher
        norm_next = norm_now - 2.0 * step_size * cross + step_size * step_size * fisher_square
        direction = residual_next + norm_next / norm_now * direction
        return (solution_now, residual_next, direction)

    solution_now, residual, _ = lax.fori_loop(
        0, ITERS, iterate, (jnp.zeros_like(residual), residual, residual)
    )
    return (
        solution_now[:, :width],
        solution_now[:, width:].T,
        residual[:, :width],
        residual[:, width:].T,
    )


def solution(mesh):
    return jax.shard_map(
        on_device,
        mesh=mesh,
        in_specs=(
            P("dp", None),
            P(None, "fsdp"),
            P("fsdp", None),
            P(),
            P(None, "fsdp"),
            P("fsdp", None),
        ),
        out_specs=(P(None, "fsdp"), P("fsdp", None), P(None, "fsdp"), P("fsdp", None)),
        check_vma=False,
    )
```

```python
import jax
import jax.numpy as jnp
from jax import lax
from jax.sharding import PartitionSpec as P

ITERS = 3


damping = 0.2
norm_eps = 1e-05


def silu_slope(preact):
    gating = jax.nn.sigmoid(preact)
    return gating * (1.0 + preact * (1.0 - gating))


def contract_rows(left_side, right_side):
    return lax.dot_general(
        left_side, right_side, (((0,), (0,)), ((), ())), preferred_element_type=jnp.float32
    )


def xor_pairs(size, bit):
    return [(i, i ^ bit) for i in range(size)]


def stages_of(size):
    count = size.bit_length() - 1
    assert 1 << count == size
    return count


def scalar_sum(values, axis):
    names = axis if isinstance(axis, tuple) else (axis,)
    size = 1
    for name in names:
        size *= lax.axis_size(name)
    gathered = lax.all_to_all(jnp.broadcast_to(values[None], (size,) + values.shape), axis, 0, 0)
    return jnp.sum(gathered, axis=0)


def digit_groups(size, first_bits):
    count = stages_of(size)
    groups = [(0, min(first_bits, count))]
    if count > first_bits:
        groups.append((first_bits, count - first_bits))
    return groups


def spread_reduce(value, axis, groups, send_type):
    size = lax.axis_size(axis)
    index = lax.axis_index(axis)
    kept = value.astype(jnp.float32)
    for low, bits in groups:
        width = 1 << bits
        digit = (index >> low) & (width - 1)
        rows = kept.shape[0] // width
        total = lax.dynamic_slice_in_dim(kept, digit * rows, rows, 0)
        for offset in range(1, width):
            send = lax.dynamic_slice_in_dim(kept, (digit ^ offset) * rows, rows, 0)
            got = lax.ppermute(send.astype(send_type), axis, xor_pairs(size, offset << low))
            total = total + got.astype(jnp.float32)
        kept = total
    return kept


def spread_gather(chunk, axis, groups):
    size = lax.axis_size(axis)
    index = lax.axis_index(axis)
    for low, bits in reversed(groups):
        width = 1 << bits
        digit = (index >> low) & (width - 1)
        rows = chunk.shape[0]
        whole = jnp.zeros((rows * width,) + chunk.shape[1:], chunk.dtype)
        whole = lax.dynamic_update_slice_in_dim(whole, chunk, digit * rows, 0)
        for offset in range(1, width):
            got = lax.ppermute(chunk, axis, xor_pairs(size, offset << low))
            whole = lax.dynamic_update_slice_in_dim(whole, got, (digit ^ offset) * rows, 0)
        chunk = whole
    return chunk


def fisher_product(direction, residual, normed, hidden_act, slope_act, w_out, metric, width):
    tangent = direction.astype(jnp.bfloat16)
    tangent_in = tangent[:, :width]
    tangent_out_t = tangent[:, width:]

    def block_term(start, rows):
        normed_rows = lax.dynamic_slice_in_dim(normed, start, rows, 0)
        slope_rows = lax.dynamic_slice_in_dim(slope_act, start, rows, 0)
        hidden_rows = lax.dynamic_slice_in_dim(hidden_act, start, rows, 0)
        pre_tangent = jnp.dot(normed_rows, tangent_in, preferred_element_type=jnp.float32)
        inner_tangent = (slope_rows * pre_tangent).astype(jnp.bfloat16)
        term = jnp.dot(inner_tangent, w_out, preferred_element_type=jnp.float32)
        term = term + lax.dot_general(
            hidden_rows, tangent_out_t, (((1,), (1,)), ((), ())), preferred_element_type=jnp.float32
        )
        return term.astype(jnp.bfloat16)

    fsdp_size = lax.axis_size("fsdp")
    fsdp_groups = digit_groups(fsdp_size, 2)
    (low, bits), later_groups = fsdp_groups[0], fsdp_groups[1:]
    group = 1 << bits
    digit = (lax.axis_index("fsdp") >> low) & (group - 1)
    rows = normed.shape[0] // group
    received = []
    for offset in range(1, group):
        send = block_term((digit ^ offset) * rows, rows)
        received.append(lax.ppermute(send, "fsdp", xor_pairs(fsdp_size, offset << low)))
    out_chunk = block_term(digit * rows, rows).astype(jnp.float32)
    for got in received:
        out_chunk = out_chunk + got.astype(jnp.float32)
    if later_groups:
        out_chunk = spread_reduce(out_chunk, "fsdp", later_groups, jnp.bfloat16)
    cotangent = spread_gather((out_chunk * metric).astype(jnp.bfloat16), "fsdp", fsdp_groups)
    back_act = lax.dot_general(
        cotangent, w_out, (((1,), (1,)), ((), ())), preferred_element_type=jnp.float32
    )
    grad_pre = (slope_act * back_act).astype(jnp.bfloat16)
    part_out_t = contract_rows(cotangent, hidden_act)
    part_in = contract_rows(normed, grad_pre)
    dp_groups = digit_groups(lax.axis_size("dp"), 3)
    reduced = spread_reduce(jnp.concatenate([part_in, part_out_t], axis=1), "dp", dp_groups, jnp.float32)
    rows = reduced.shape[0]
    start = lax.axis_index("dp") * rows
    direction_chunk = lax.dynamic_slice_in_dim(direction, start, rows, 0)
    residual_chunk = lax.dynamic_slice_in_dim(residual, start, rows, 0)
    fisher_chunk = reduced + damping * direction_chunk
    sums = jnp.stack(
        [
            jnp.sum(direction_chunk * fisher_chunk),
            jnp.sum(residual_chunk * fisher_chunk),
            jnp.sum(fisher_chunk * fisher_chunk),
            jnp.sum(residual_chunk * residual_chunk),
        ]
    )
    fisher = spread_gather(fisher_chunk, "dp", dp_groups)
    return fisher, scalar_sum(sums, ("dp", "fsdp"))


def on_device(states, w_in, w_out, precision, grad_in, grad_out):
    row_count = states.shape[0]
    width = w_in.shape[1]
    metric = precision / (row_count * lax.axis_size("dp"))
    wide_states = states.astype(jnp.float32)
    mean_square = jnp.mean(wide_states * wide_states, axis=1, keepdims=True)
    normed = (wide_states * lax.rsqrt(mean_square + norm_eps)).astype(jnp.bfloat16)
    preact = jnp.dot(normed, w_in, preferred_element_type=jnp.float32)
    hidden_act = jax.nn.silu(preact).astype(jnp.bfloat16)
    slope_act = silu_slope(preact)
    residual = jnp.concatenate([grad_in, grad_out.T], axis=1)

    def iterate(_, carry):
        solution_now, residual, direction = carry
        fisher, sums = fisher_product(
            direction, residual, normed, hidden_act, slope_act, w_out, metric, width
        )
        quadratic, cross, fisher_square, norm_now = sums
        step_size = norm_now / quadratic
        solution_now = solution_now + step_size * direction
        residual_next = residual - step_size * fisher
        norm_next = norm_now - 2.0 * step_size * cross + step_size * step_size * fisher_square
        direction = residual_next + norm_next / norm_now * direction
        return (solution_now, residual_next, direction)

    solution_now, residual, _ = lax.fori_loop(
        0, ITERS, iterate, (jnp.zeros_like(residual), residual, residual)
    )
    return (
        solution_now[:, :width],
        solution_now[:, width:].T,
        residual[:, :width],
        residual[:, width:].T,
    )


def solution(mesh):
    return jax.shard_map(
        on_device,
        mesh=mesh,
        in_specs=(
            P("dp", None),
            P(None, "fsdp"),
            P("fsdp", None),
            P(),
            P(None, "fsdp"),
            P("fsdp", None),
        ),
        out_specs=(P(None, "fsdp"), P("fsdp", None), P(None, "fsdp"), P("fsdp", None)),
        check_vma=False,
    )
```

```python
import jax
import jax.numpy as jnp
from jax import lax
from jax.sharding import PartitionSpec as P

ITERS = 3


damping = 0.2
norm_eps = 1e-05


def silu_slope(preact):
    gating = jax.nn.sigmoid(preact)
    return gating * (1.0 + preact * (1.0 - gating))


def contract_rows(left_side, right_side):
    return lax.dot_general(
        left_side, right_side, (((0,), (0,)), ((), ())), preferred_element_type=jnp.float32
    )


def xor_pairs(size, bit):
    return [(i, i ^ bit) for i in range(size)]


def stages_of(size):
    count = size.bit_length() - 1
    assert 1 << count == size
    return count


def scalar_sum(values, axis):
    names = axis if isinstance(axis, tuple) else (axis,)
    size = 1
    for name in names:
        size *= lax.axis_size(name)
    gathered = lax.all_to_all(jnp.broadcast_to(values[None], (size,) + values.shape), axis, 0, 0)
    return jnp.sum(gathered, axis=0)


def digit_groups(size, first_bits):
    count = stages_of(size)
    groups = [(0, min(first_bits, count))]
    if count > first_bits:
        groups.append((first_bits, count - first_bits))
    return groups


def spread_reduce(value, axis, groups, send_type):
    size = lax.axis_size(axis)
    index = lax.axis_index(axis)
    kept = value.astype(jnp.float32)
    for low, bits in groups:
        width = 1 << bits
        digit = (index >> low) & (width - 1)
        rows = kept.shape[0] // width
        total = lax.dynamic_slice_in_dim(kept, digit * rows, rows, 0)
        for offset in range(1, width):
            send = lax.dynamic_slice_in_dim(kept, (digit ^ offset) * rows, rows, 0)
            got = lax.ppermute(send.astype(send_type), axis, xor_pairs(size, offset << low))
            total = total + got.astype(jnp.float32)
        kept = total
    return kept


def spread_gather(chunk, axis, groups):
    size = lax.axis_size(axis)
    index = lax.axis_index(axis)
    for low, bits in reversed(groups):
        width = 1 << bits
        digit = (index >> low) & (width - 1)
        rows = chunk.shape[0]
        whole = jnp.zeros((rows * width,) + chunk.shape[1:], chunk.dtype)
        whole = lax.dynamic_update_slice_in_dim(whole, chunk, digit * rows, 0)
        for offset in range(1, width):
            got = lax.ppermute(chunk, axis, xor_pairs(size, offset << low))
            whole = lax.dynamic_update_slice_in_dim(whole, got, (digit ^ offset) * rows, 0)
        chunk = whole
    return chunk


def xor_arrange(value, axis, groups):
    if not groups:
        return value
    (low, bits), rest = groups[0], groups[1:]
    width = 1 << bits
    digit = (lax.axis_index(axis) >> low) & (width - 1)
    rows = value.shape[0] // width
    return jnp.concatenate(
        [
            xor_arrange(lax.dynamic_slice_in_dim(value, (digit ^ p) * rows, rows, 0), axis, rest)
            for p in range(width)
        ],
        axis=0,
    )


def arranged_reduce(value, axis, groups, send_type):
    size = lax.axis_size(axis)
    kept = value.astype(jnp.float32)
    for low, bits in groups:
        width = 1 << bits
        rows = kept.shape[0] // width
        total = kept[:rows]
        for offset in range(1, width):
            send = kept[offset * rows : (offset + 1) * rows]
            got = lax.ppermute(send.astype(send_type), axis, xor_pairs(size, offset << low))
            total = total + got.astype(jnp.float32)
        kept = total
    return kept


def arranged_gather(chunk, axis, groups):
    size = lax.axis_size(axis)
    for low, bits in reversed(groups):
        width = 1 << bits
        pieces = [chunk] + [
            lax.ppermute(chunk, axis, xor_pairs(size, offset << low)) for offset in range(1, width)
        ]
        chunk = jnp.concatenate(pieces, axis=0)
    return chunk


def fisher_product(direction, residual, normed, hidden_act, slope_act, w_out, metric, width):
    tangent = direction.astype(jnp.bfloat16)
    tangent_in = tangent[:, :width]
    tangent_out_t = tangent[:, width:]
    pre_tangent = jnp.dot(normed, tangent_in, preferred_element_type=jnp.float32)
    inner_tangent = (slope_act * pre_tangent).astype(jnp.bfloat16)
    partial_out = jnp.dot(inner_tangent, w_out, preferred_element_type=jnp.float32)
    partial_out = partial_out + lax.dot_general(
        hidden_act, tangent_out_t, (((1,), (1,)), ((), ())), preferred_element_type=jnp.float32
    )
    fsdp_groups = digit_groups(lax.axis_size("fsdp"), 2)
    out_chunk = arranged_reduce(partial_out.astype(jnp.bfloat16), "fsdp", fsdp_groups, jnp.bfloat16)
    cotangent = arranged_gather((out_chunk * metric).astype(jnp.bfloat16), "fsdp", fsdp_groups)
    back_act = lax.dot_general(
        cotangent, w_out, (((1,), (1,)), ((), ())), preferred_element_type=jnp.float32
    )
    grad_pre = (slope_act * back_act).astype(jnp.bfloat16)
    part_out_t = contract_rows(cotangent, hidden_act)
    part_in = contract_rows(normed, grad_pre)
    dp_groups = digit_groups(lax.axis_size("dp"), 3)
    reduced = spread_reduce(jnp.concatenate([part_in, part_out_t], axis=1), "dp", dp_groups, jnp.float32)
    rows = reduced.shape[0]
    start = lax.axis_index("dp") * rows
    direction_chunk = lax.dynamic_slice_in_dim(direction, start, rows, 0)
    residual_chunk = lax.dynamic_slice_in_dim(residual, start, rows, 0)
    fisher_chunk = reduced + damping * direction_chunk
    sums = jnp.stack(
        [
            jnp.sum(direction_chunk * fisher_chunk),
            jnp.sum(residual_chunk * fisher_chunk),
            jnp.sum(fisher_chunk * fisher_chunk),
            jnp.sum(residual_chunk * residual_chunk),
        ]
    )
    fisher = spread_gather(fisher_chunk, "dp", dp_groups)
    return fisher, scalar_sum(sums, ("dp", "fsdp"))


def on_device(states, w_in, w_out, precision, grad_in, grad_out):
    row_count = states.shape[0]
    width = w_in.shape[1]
    metric = precision / (row_count * lax.axis_size("dp"))
    wide_states = states.astype(jnp.float32)
    mean_square = jnp.mean(wide_states * wide_states, axis=1, keepdims=True)
    normed = (wide_states * lax.rsqrt(mean_square + norm_eps)).astype(jnp.bfloat16)
    preact = jnp.dot(normed, w_in, preferred_element_type=jnp.float32)
    hidden_act = jax.nn.silu(preact).astype(jnp.bfloat16)
    slope_act = silu_slope(preact)
    fsdp_groups = digit_groups(lax.axis_size("fsdp"), 2)
    normed, hidden_act, slope_act = (
        xor_arrange(value, "fsdp", fsdp_groups) for value in (normed, hidden_act, slope_act)
    )
    residual = jnp.concatenate([grad_in, grad_out.T], axis=1)

    def iterate(_, carry):
        solution_now, residual, direction = carry
        fisher, sums = fisher_product(
            direction, residual, normed, hidden_act, slope_act, w_out, metric, width
        )
        quadratic, cross, fisher_square, norm_now = sums
        step_size = norm_now / quadratic
        solution_now = solution_now + step_size * direction
        residual_next = residual - step_size * fisher
        norm_next = norm_now - 2.0 * step_size * cross + step_size * step_size * fisher_square
        direction = residual_next + norm_next / norm_now * direction
        return (solution_now, residual_next, direction)

    solution_now, residual, _ = lax.fori_loop(
        0, ITERS, iterate, (jnp.zeros_like(residual), residual, residual)
    )
    return (
        solution_now[:, :width],
        solution_now[:, width:].T,
        residual[:, :width],
        residual[:, width:].T,
    )


def solution(mesh):
    return jax.shard_map(
        on_device,
        mesh=mesh,
        in_specs=(
            P("dp", None),
            P(None, "fsdp"),
            P("fsdp", None),
            P(),
            P(None, "fsdp"),
            P("fsdp", None),
        ),
        out_specs=(P(None, "fsdp"), P("fsdp", None), P(None, "fsdp"), P("fsdp", None)),
        check_vma=False,
    )
```

```python
import jax
import jax.numpy as jnp
from jax import lax
from jax.sharding import PartitionSpec as P

ITERS = 3


damping = 0.2
norm_eps = 1e-05


def silu_slope(preact):
    gating = jax.nn.sigmoid(preact)
    return gating * (1.0 + preact * (1.0 - gating))


def contract_rows(left_side, right_side):
    return lax.dot_general(
        left_side, right_side, (((0,), (0,)), ((), ())), preferred_element_type=jnp.float32
    )


def xor_pairs(size, bit):
    return [(i, i ^ bit) for i in range(size)]


def stages_of(size):
    count = size.bit_length() - 1
    assert 1 << count == size
    return count


def scalar_sum(values, axis):
    names = axis if isinstance(axis, tuple) else (axis,)
    size = 1
    for name in names:
        size *= lax.axis_size(name)
    gathered = lax.all_to_all(jnp.broadcast_to(values[None], (size,) + values.shape), axis, 0, 0)
    return jnp.sum(gathered, axis=0)


def digit_groups(size, widths):
    count = stages_of(size)
    groups, low = [], 0
    for bits in widths:
        if low >= count:
            break
        groups.append((low, min(bits, count - low)))
        low += groups[-1][1]
    if low < count:
        groups.append((low, count - low))
    return groups


def spread_reduce(value, axis, groups, send_type):
    size = lax.axis_size(axis)
    index = lax.axis_index(axis)
    kept = value.astype(jnp.float32)
    for low, bits in groups:
        width = 1 << bits
        digit = (index >> low) & (width - 1)
        rows = kept.shape[0] // width
        total = lax.dynamic_slice_in_dim(kept, digit * rows, rows, 0)
        for offset in range(1, width):
            send = lax.dynamic_slice_in_dim(kept, (digit ^ offset) * rows, rows, 0)
            got = lax.ppermute(send.astype(send_type), axis, xor_pairs(size, offset << low))
            total = total + got.astype(jnp.float32)
        kept = total
    return kept


def spread_gather(chunk, axis, groups):
    size = lax.axis_size(axis)
    index = lax.axis_index(axis)
    for low, bits in reversed(groups):
        width = 1 << bits
        digit = (index >> low) & (width - 1)
        rows = chunk.shape[0]
        whole = jnp.zeros((rows * width,) + chunk.shape[1:], chunk.dtype)
        whole = lax.dynamic_update_slice_in_dim(whole, chunk, digit * rows, 0)
        for offset in range(1, width):
            got = lax.ppermute(chunk, axis, xor_pairs(size, offset << low))
            whole = lax.dynamic_update_slice_in_dim(whole, got, (digit ^ offset) * rows, 0)
        chunk = whole
    return chunk


def fisher_product(direction, residual, normed, hidden_act, slope_act, w_out, metric, width):
    tangent = direction.astype(jnp.bfloat16)
    tangent_in = tangent[:, :width]
    tangent_out_t = tangent[:, width:]
    pre_tangent = jnp.dot(normed, tangent_in, preferred_element_type=jnp.float32)
    inner_tangent = (slope_act * pre_tangent).astype(jnp.bfloat16)
    partial_out = jnp.dot(inner_tangent, w_out, preferred_element_type=jnp.float32)
    partial_out = partial_out + lax.dot_general(
        hidden_act, tangent_out_t, (((1,), (1,)), ((), ())), preferred_element_type=jnp.float32
    )
    fsdp_groups = digit_groups(lax.axis_size("fsdp"), (1, 1))
    out_chunk = spread_reduce(partial_out.astype(jnp.bfloat16), "fsdp", fsdp_groups, jnp.bfloat16)
    cotangent = spread_gather((out_chunk * metric).astype(jnp.bfloat16), "fsdp", fsdp_groups)
    back_act = lax.dot_general(
        cotangent, w_out, (((1,), (1,)), ((), ())), preferred_element_type=jnp.float32
    )
    grad_pre = (slope_act * back_act).astype(jnp.bfloat16)
    part_out_t = contract_rows(cotangent, hidden_act)
    part_in = contract_rows(normed, grad_pre)
    dp_groups = digit_groups(lax.axis_size("dp"), (3,))
    reduced = spread_reduce(jnp.concatenate([part_in, part_out_t], axis=1), "dp", dp_groups, jnp.float32)
    rows = reduced.shape[0]
    start = lax.axis_index("dp") * rows
    direction_chunk = lax.dynamic_slice_in_dim(direction, start, rows, 0)
    residual_chunk = lax.dynamic_slice_in_dim(residual, start, rows, 0)
    fisher_chunk = reduced + damping * direction_chunk
    sums = jnp.stack(
        [
            jnp.sum(direction_chunk * fisher_chunk),
            jnp.sum(residual_chunk * fisher_chunk),
            jnp.sum(fisher_chunk * fisher_chunk),
            jnp.sum(residual_chunk * residual_chunk),
        ]
    )
    fisher = spread_gather(fisher_chunk, "dp", dp_groups)
    return fisher, scalar_sum(sums, ("dp", "fsdp"))


def on_device(states, w_in, w_out, precision, grad_in, grad_out):
    row_count = states.shape[0]
    width = w_in.shape[1]
    metric = precision / (row_count * lax.axis_size("dp"))
    wide_states = states.astype(jnp.float32)
    mean_square = jnp.mean(wide_states * wide_states, axis=1, keepdims=True)
    normed = (wide_states * lax.rsqrt(mean_square + norm_eps)).astype(jnp.bfloat16)
    preact = jnp.dot(normed, w_in, preferred_element_type=jnp.float32)
    hidden_act = jax.nn.silu(preact).astype(jnp.bfloat16)
    slope_act = silu_slope(preact)
    residual = jnp.concatenate([grad_in, grad_out.T], axis=1)

    def iterate(_, carry):
        solution_now, residual, direction = carry
        fisher, sums = fisher_product(
            direction, residual, normed, hidden_act, slope_act, w_out, metric, width
        )
        quadratic, cross, fisher_square, norm_now = sums
        step_size = norm_now / quadratic
        solution_now = solution_now + step_size * direction
        residual_next = residual - step_size * fisher
        norm_next = norm_now - 2.0 * step_size * cross + step_size * step_size * fisher_square
        direction = residual_next + norm_next / norm_now * direction
        return (solution_now, residual_next, direction)

    solution_now, residual, _ = lax.fori_loop(
        0, ITERS, iterate, (jnp.zeros_like(residual), residual, residual)
    )
    return (
        solution_now[:, :width],
        solution_now[:, width:].T,
        residual[:, :width],
        residual[:, width:].T,
    )


def solution(mesh):
    return jax.shard_map(
        on_device,
        mesh=mesh,
        in_specs=(
            P("dp", None),
            P(None, "fsdp"),
            P("fsdp", None),
            P(),
            P(None, "fsdp"),
            P("fsdp", None),
        ),
        out_specs=(P(None, "fsdp"), P("fsdp", None), P(None, "fsdp"), P("fsdp", None)),
        check_vma=False,
    )
```

```python
import jax
import jax.numpy as jnp
from jax import lax
from jax.sharding import PartitionSpec as P

ITERS = 3


damping = 0.2
norm_eps = 1e-05


def silu_slope(preact):
    gating = jax.nn.sigmoid(preact)
    return gating * (1.0 + preact * (1.0 - gating))


def contract_rows(left_side, right_side):
    return lax.dot_general(
        left_side, right_side, (((0,), (0,)), ((), ())), preferred_element_type=jnp.float32
    )


def xor_pairs(size, bit):
    return [(i, i ^ bit) for i in range(size)]


def stages_of(size):
    count = size.bit_length() - 1
    assert 1 << count == size
    return count


def scalar_sum(values, axis):
    names = axis if isinstance(axis, tuple) else (axis,)
    size = 1
    for name in names:
        size *= lax.axis_size(name)
    gathered = lax.all_to_all(jnp.broadcast_to(values[None], (size,) + values.shape), axis, 0, 0)
    return jnp.sum(gathered, axis=0)


def digit_groups(size, widths):
    count = stages_of(size)
    groups, low = [], 0
    for bits in widths:
        if low >= count:
            break
        groups.append((low, min(bits, count - low)))
        low += groups[-1][1]
    if low < count:
        groups.append((low, count - low))
    return groups


def chunk_position(axis, groups):
    index = lax.axis_index(axis)
    position = 0
    for low, bits in groups:
        position = position * (1 << bits) + ((index >> low) & ((1 << bits) - 1))
    return position


def spread_reduce(value, axis, groups, send_type):
    size = lax.axis_size(axis)
    index = lax.axis_index(axis)
    kept = value.astype(jnp.float32)
    for low, bits in groups:
        width = 1 << bits
        digit = (index >> low) & (width - 1)
        rows = kept.shape[0] // width
        total = lax.dynamic_slice_in_dim(kept, digit * rows, rows, 0)
        for offset in range(1, width):
            send = lax.dynamic_slice_in_dim(kept, (digit ^ offset) * rows, rows, 0)
            got = lax.ppermute(send.astype(send_type), axis, xor_pairs(size, offset << low))
            total = total + got.astype(jnp.float32)
        kept = total
    return kept


def spread_gather(chunk, axis, groups):
    size = lax.axis_size(axis)
    index = lax.axis_index(axis)
    for low, bits in reversed(groups):
        width = 1 << bits
        digit = (index >> low) & (width - 1)
        rows = chunk.shape[0]
        whole = jnp.zeros((rows * width,) + chunk.shape[1:], chunk.dtype)
        whole = lax.dynamic_update_slice_in_dim(whole, chunk, digit * rows, 0)
        for offset in range(1, width):
            got = lax.ppermute(chunk, axis, xor_pairs(size, offset << low))
            whole = lax.dynamic_update_slice_in_dim(whole, got, (digit ^ offset) * rows, 0)
        chunk = whole
    return chunk


def fisher_product(direction, residual, normed, hidden_act, slope_act, w_out, metric, width):
    tangent = direction.astype(jnp.bfloat16)
    tangent_in = tangent[:, :width]
    tangent_out_t = tangent[:, width:]
    pre_tangent = jnp.dot(normed, tangent_in, preferred_element_type=jnp.float32)
    inner_tangent = (slope_act * pre_tangent).astype(jnp.bfloat16)
    partial_out = jnp.dot(inner_tangent, w_out, preferred_element_type=jnp.float32)
    partial_out = partial_out + lax.dot_general(
        hidden_act, tangent_out_t, (((1,), (1,)), ((), ())), preferred_element_type=jnp.float32
    )
    fsdp_groups = digit_groups(lax.axis_size("fsdp"), (1, 1))
    out_chunk = spread_reduce(partial_out.astype(jnp.bfloat16), "fsdp", fsdp_groups, jnp.bfloat16)
    cotangent = spread_gather((out_chunk * metric).astype(jnp.bfloat16), "fsdp", fsdp_groups)
    back_act = lax.dot_general(
        cotangent, w_out, (((1,), (1,)), ((), ())), preferred_element_type=jnp.float32
    )
    grad_pre = (slope_act * back_act).astype(jnp.bfloat16)
    part_out_t = contract_rows(cotangent, hidden_act)
    part_in = contract_rows(normed, grad_pre)
    dp_groups = digit_groups(lax.axis_size("dp"), (2, 1))
    reduced = spread_reduce(jnp.concatenate([part_in, part_out_t], axis=1), "dp", dp_groups, jnp.float32)
    rows = reduced.shape[0]
    start = chunk_position("dp", dp_groups) * rows
    direction_chunk = lax.dynamic_slice_in_dim(direction, start, rows, 0)
    residual_chunk = lax.dynamic_slice_in_dim(residual, start, rows, 0)
    fisher_chunk = reduced + damping * direction_chunk
    sums = jnp.stack(
        [
            jnp.sum(direction_chunk * fisher_chunk),
            jnp.sum(residual_chunk * fisher_chunk),
            jnp.sum(fisher_chunk * fisher_chunk),
            jnp.sum(residual_chunk * residual_chunk),
        ]
    )
    fisher = spread_gather(fisher_chunk, "dp", dp_groups)
    return fisher, scalar_sum(sums, ("dp", "fsdp"))


def on_device(states, w_in, w_out, precision, grad_in, grad_out):
    row_count = states.shape[0]
    width = w_in.shape[1]
    metric = precision / (row_count * lax.axis_size("dp"))
    wide_states = states.astype(jnp.float32)
    mean_square = jnp.mean(wide_states * wide_states, axis=1, keepdims=True)
    normed = (wide_states * lax.rsqrt(mean_square + norm_eps)).astype(jnp.bfloat16)
    preact = jnp.dot(normed, w_in, preferred_element_type=jnp.float32)
    hidden_act = jax.nn.silu(preact).astype(jnp.bfloat16)
    slope_act = silu_slope(preact)
    residual = jnp.concatenate([grad_in, grad_out.T], axis=1)

    def iterate(_, carry):
        solution_now, residual, direction = carry
        fisher, sums = fisher_product(
            direction, residual, normed, hidden_act, slope_act, w_out, metric, width
        )
        quadratic, cross, fisher_square, norm_now = sums
        step_size = norm_now / quadratic
        solution_now = solution_now + step_size * direction
        residual_next = residual - step_size * fisher
        norm_next = norm_now - 2.0 * step_size * cross + step_size * step_size * fisher_square
        direction = residual_next + norm_next / norm_now * direction
        return (solution_now, residual_next, direction)

    solution_now, residual, _ = lax.fori_loop(
        0, ITERS, iterate, (jnp.zeros_like(residual), residual, residual)
    )
    return (
        solution_now[:, :width],
        solution_now[:, width:].T,
        residual[:, :width],
        residual[:, width:].T,
    )


def solution(mesh):
    return jax.shard_map(
        on_device,
        mesh=mesh,
        in_specs=(
            P("dp", None),
            P(None, "fsdp"),
            P("fsdp", None),
            P(),
            P(None, "fsdp"),
            P("fsdp", None),
        ),
        out_specs=(P(None, "fsdp"), P("fsdp", None), P(None, "fsdp"), P("fsdp", None)),
        check_vma=False,
    )
```

```python
import jax
import jax.numpy as jnp
from jax import lax
from jax.sharding import PartitionSpec as P

ITERS = 3


damping = 0.2
norm_eps = 1e-05


def silu_slope(preact):
    gating = jax.nn.sigmoid(preact)
    return gating * (1.0 + preact * (1.0 - gating))


def contract_rows(left_side, right_side):
    return lax.dot_general(
        left_side, right_side, (((0,), (0,)), ((), ())), preferred_element_type=jnp.float32
    )


def xor_pairs(size, bit):
    return [(i, i ^ bit) for i in range(size)]


def stages_of(size):
    count = size.bit_length() - 1
    assert 1 << count == size
    return count


def scalar_sum(values, axis):
    names = axis if isinstance(axis, tuple) else (axis,)
    size = 1
    for name in names:
        size *= lax.axis_size(name)
    gathered = lax.all_to_all(jnp.broadcast_to(values[None], (size,) + values.shape), axis, 0, 0)
    return jnp.sum(gathered, axis=0)


def digit_groups(size, widths):
    count = stages_of(size)
    groups, low = [], 0
    for bits in widths:
        if low >= count:
            break
        groups.append((low, min(bits, count - low)))
        low += groups[-1][1]
    if low < count:
        groups.append((low, count - low))
    return groups


def spread_reduce(value, axis, groups, send_type):
    size = lax.axis_size(axis)
    index = lax.axis_index(axis)
    kept = value.astype(jnp.float32)
    for low, bits in groups:
        width = 1 << bits
        digit = (index >> low) & (width - 1)
        rows = kept.shape[0] // width
        total = lax.dynamic_slice_in_dim(kept, digit * rows, rows, 0)
        for offset in range(1, width):
            send = lax.dynamic_slice_in_dim(kept, (digit ^ offset) * rows, rows, 0)
            got = lax.ppermute(send.astype(send_type), axis, xor_pairs(size, offset << low))
            total = total + got.astype(jnp.float32)
        kept = total
    return kept


def spread_gather(chunk, axis, groups):
    size = lax.axis_size(axis)
    index = lax.axis_index(axis)
    for low, bits in reversed(groups):
        width = 1 << bits
        digit = (index >> low) & (width - 1)
        rows = chunk.shape[0]
        whole = jnp.zeros((rows * width,) + chunk.shape[1:], chunk.dtype)
        whole = lax.dynamic_update_slice_in_dim(whole, chunk, digit * rows, 0)
        for offset in range(1, width):
            got = lax.ppermute(chunk, axis, xor_pairs(size, offset << low))
            whole = lax.dynamic_update_slice_in_dim(whole, got, (digit ^ offset) * rows, 0)
        chunk = whole
    return chunk


def fisher_product(direction, residual, normed, hidden_act, slope_act, w_out, metric, width):
    tangent = direction.astype(jnp.bfloat16)
    tangent_in = tangent[:, :width]
    tangent_out_t = tangent[:, width:]
    pre_tangent = jnp.dot(normed, tangent_in, preferred_element_type=jnp.float32)
    inner_tangent = (slope_act * pre_tangent).astype(jnp.bfloat16)
    partial_out = jnp.dot(inner_tangent, w_out, preferred_element_type=jnp.float32)
    partial_out = partial_out + lax.dot_general(
        hidden_act, tangent_out_t, (((1,), (1,)), ((), ())), preferred_element_type=jnp.float32
    )
    fsdp_groups = digit_groups(lax.axis_size("fsdp"), (1, 1, 2))
    out_chunk = spread_reduce(partial_out.astype(jnp.bfloat16), "fsdp", fsdp_groups, jnp.bfloat16)
    cotangent = spread_gather((out_chunk * metric).astype(jnp.bfloat16), "fsdp", fsdp_groups)
    back_act = lax.dot_general(
        cotangent, w_out, (((1,), (1,)), ((), ())), preferred_element_type=jnp.float32
    )
    grad_pre = (slope_act * back_act).astype(jnp.bfloat16)
    part_out_t = contract_rows(cotangent, hidden_act)
    part_in = contract_rows(normed, grad_pre)
    dp_groups = digit_groups(lax.axis_size("dp"), (3,))
    reduced = spread_reduce(jnp.concatenate([part_in, part_out_t], axis=1), "dp", dp_groups, jnp.float32)
    rows = reduced.shape[0]
    start = lax.axis_index("dp") * rows
    direction_chunk = lax.dynamic_slice_in_dim(direction, start, rows, 0)
    residual_chunk = lax.dynamic_slice_in_dim(residual, start, rows, 0)
    fisher_chunk = reduced + damping * direction_chunk
    sums = jnp.stack(
        [
            jnp.sum(direction_chunk * fisher_chunk),
            jnp.sum(residual_chunk * fisher_chunk),
            jnp.sum(fisher_chunk * fisher_chunk),
            jnp.sum(residual_chunk * residual_chunk),
        ]
    )
    fisher = spread_gather(fisher_chunk, "dp", dp_groups)
    return fisher, scalar_sum(sums, ("dp", "fsdp"))


def on_device(states, w_in, w_out, precision, grad_in, grad_out):
    row_count = states.shape[0]
    width = w_in.shape[1]
    metric = precision / (row_count * lax.axis_size("dp"))
    wide_states = states.astype(jnp.float32)
    mean_square = jnp.mean(wide_states * wide_states, axis=1, keepdims=True)
    normed = (wide_states * lax.rsqrt(mean_square + norm_eps)).astype(jnp.bfloat16)
    preact = jnp.dot(normed, w_in, preferred_element_type=jnp.float32)
    hidden_act = jax.nn.silu(preact).astype(jnp.bfloat16)
    slope_act = silu_slope(preact)
    residual = jnp.concatenate([grad_in, grad_out.T], axis=1)

    def iterate(_, carry):
        solution_now, residual, direction = carry
        fisher, sums = fisher_product(
            direction, residual, normed, hidden_act, slope_act, w_out, metric, width
        )
        quadratic, cross, fisher_square, norm_now = sums
        step_size = norm_now / quadratic
        solution_now = solution_now + step_size * direction
        residual_next = residual - step_size * fisher
        norm_next = norm_now - 2.0 * step_size * cross + step_size * step_size * fisher_square
        direction = residual_next + norm_next / norm_now * direction
        return (solution_now, residual_next, direction)

    solution_now, residual, _ = lax.fori_loop(
        0, ITERS, iterate, (jnp.zeros_like(residual), residual, residual)
    )
    return (
        solution_now[:, :width],
        solution_now[:, width:].T,
        residual[:, :width],
        residual[:, width:].T,
    )


def solution(mesh):
    return jax.shard_map(
        on_device,
        mesh=mesh,
        in_specs=(
            P("dp", None),
            P(None, "fsdp"),
            P("fsdp", None),
            P(),
            P(None, "fsdp"),
            P("fsdp", None),
        ),
        out_specs=(P(None, "fsdp"), P("fsdp", None), P(None, "fsdp"), P("fsdp", None)),
        check_vma=False,
    )
```

```python
import jax
import jax.numpy as jnp
from jax import lax
from jax.sharding import PartitionSpec as P

ITERS = 3


damping = 0.2
norm_eps = 1e-05


def silu_slope(preact):
    gating = jax.nn.sigmoid(preact)
    return gating * (1.0 + preact * (1.0 - gating))


def contract_rows(left_side, right_side):
    return lax.dot_general(
        left_side, right_side, (((0,), (0,)), ((), ())), preferred_element_type=jnp.float32
    )


def xor_pairs(size, bit):
    return [(i, i ^ bit) for i in range(size)]


def stages_of(size):
    count = size.bit_length() - 1
    assert 1 << count == size
    return count


def scalar_sum(values, axis):
    names = axis if isinstance(axis, tuple) else (axis,)
    size = 1
    for name in names:
        size *= lax.axis_size(name)
    gathered = lax.all_to_all(jnp.broadcast_to(values[None], (size,) + values.shape), axis, 0, 0)
    return jnp.sum(gathered, axis=0)


def digit_groups(size, widths):
    count = stages_of(size)
    groups, low = [], 0
    for bits in widths:
        if low >= count:
            break
        groups.append((low, min(bits, count - low)))
        low += groups[-1][1]
    if low < count:
        groups.append((low, count - low))
    return groups


def split_permute(value, axis, pairs):
    if value.shape[0] < 192:
        return lax.ppermute(value, axis, pairs)
    upper, lower = jnp.split(value, 2, axis=0)
    return jnp.concatenate([lax.ppermute(upper, axis, pairs), lax.ppermute(lower, axis, pairs)], 0)


def spread_reduce(value, axis, groups, send_type):
    size = lax.axis_size(axis)
    index = lax.axis_index(axis)
    kept = value.astype(jnp.float32)
    for low, bits in groups:
        width = 1 << bits
        digit = (index >> low) & (width - 1)
        rows = kept.shape[0] // width
        total = lax.dynamic_slice_in_dim(kept, digit * rows, rows, 0)
        for offset in range(1, width):
            send = lax.dynamic_slice_in_dim(kept, (digit ^ offset) * rows, rows, 0)
            got = split_permute(send.astype(send_type), axis, xor_pairs(size, offset << low))
            total = total + got.astype(jnp.float32)
        kept = total
    return kept


def spread_gather(chunk, axis, groups):
    size = lax.axis_size(axis)
    index = lax.axis_index(axis)
    for low, bits in reversed(groups):
        width = 1 << bits
        digit = (index >> low) & (width - 1)
        rows = chunk.shape[0]
        whole = jnp.zeros((rows * width,) + chunk.shape[1:], chunk.dtype)
        whole = lax.dynamic_update_slice_in_dim(whole, chunk, digit * rows, 0)
        for offset in range(1, width):
            got = split_permute(chunk, axis, xor_pairs(size, offset << low))
            whole = lax.dynamic_update_slice_in_dim(whole, got, (digit ^ offset) * rows, 0)
        chunk = whole
    return chunk


def fisher_product(direction, residual, normed, hidden_act, slope_act, w_out, metric, width):
    tangent = direction.astype(jnp.bfloat16)
    tangent_in = tangent[:, :width]
    tangent_out_t = tangent[:, width:]
    pre_tangent = jnp.dot(normed, tangent_in, preferred_element_type=jnp.float32)
    inner_tangent = (slope_act * pre_tangent).astype(jnp.bfloat16)
    partial_out = jnp.dot(inner_tangent, w_out, preferred_element_type=jnp.float32)
    partial_out = partial_out + lax.dot_general(
        hidden_act, tangent_out_t, (((1,), (1,)), ((), ())), preferred_element_type=jnp.float32
    )
    fsdp_groups = digit_groups(lax.axis_size("fsdp"), (1, 1, 2))
    out_chunk = spread_reduce(partial_out.astype(jnp.bfloat16), "fsdp", fsdp_groups, jnp.bfloat16)
    cotangent = spread_gather((out_chunk * metric).astype(jnp.bfloat16), "fsdp", fsdp_groups)
    back_act = lax.dot_general(
        cotangent, w_out, (((1,), (1,)), ((), ())), preferred_element_type=jnp.float32
    )
    grad_pre = (slope_act * back_act).astype(jnp.bfloat16)
    part_out_t = contract_rows(cotangent, hidden_act)
    part_in = contract_rows(normed, grad_pre)
    dp_groups = digit_groups(lax.axis_size("dp"), (3,))
    reduced = spread_reduce(jnp.concatenate([part_in, part_out_t], axis=1), "dp", dp_groups, jnp.float32)
    rows = reduced.shape[0]
    start = lax.axis_index("dp") * rows
    direction_chunk = lax.dynamic_slice_in_dim(direction, start, rows, 0)
    residual_chunk = lax.dynamic_slice_in_dim(residual, start, rows, 0)
    fisher_chunk = reduced + damping * direction_chunk
    sums = jnp.stack(
        [
            jnp.sum(direction_chunk * fisher_chunk),
            jnp.sum(residual_chunk * fisher_chunk),
            jnp.sum(fisher_chunk * fisher_chunk),
            jnp.sum(residual_chunk * residual_chunk),
        ]
    )
    fisher = spread_gather(fisher_chunk, "dp", dp_groups)
    return fisher, scalar_sum(sums, ("dp", "fsdp"))


def on_device(states, w_in, w_out, precision, grad_in, grad_out):
    row_count = states.shape[0]
    width = w_in.shape[1]
    metric = precision / (row_count * lax.axis_size("dp"))
    wide_states = states.astype(jnp.float32)
    mean_square = jnp.mean(wide_states * wide_states, axis=1, keepdims=True)
    normed = (wide_states * lax.rsqrt(mean_square + norm_eps)).astype(jnp.bfloat16)
    preact = jnp.dot(normed, w_in, preferred_element_type=jnp.float32)
    hidden_act = jax.nn.silu(preact).astype(jnp.bfloat16)
    slope_act = silu_slope(preact)
    residual = jnp.concatenate([grad_in, grad_out.T], axis=1)

    def iterate(_, carry):
        solution_now, residual, direction = carry
        fisher, sums = fisher_product(
            direction, residual, normed, hidden_act, slope_act, w_out, metric, width
        )
        quadratic, cross, fisher_square, norm_now = sums
        step_size = norm_now / quadratic
        solution_now = solution_now + step_size * direction
        residual_next = residual - step_size * fisher
        norm_next = norm_now - 2.0 * step_size * cross + step_size * step_size * fisher_square
        direction = residual_next + norm_next / norm_now * direction
        return (solution_now, residual_next, direction)

    solution_now, residual, _ = lax.fori_loop(
        0, ITERS, iterate, (jnp.zeros_like(residual), residual, residual)
    )
    return (
        solution_now[:, :width],
        solution_now[:, width:].T,
        residual[:, :width],
        residual[:, width:].T,
    )


def solution(mesh):
    return jax.shard_map(
        on_device,
        mesh=mesh,
        in_specs=(
            P("dp", None),
            P(None, "fsdp"),
            P("fsdp", None),
            P(),
            P(None, "fsdp"),
            P("fsdp", None),
        ),
        out_specs=(P(None, "fsdp"), P("fsdp", None), P(None, "fsdp"), P("fsdp", None)),
        check_vma=False,
    )
```

```python
import jax
import jax.numpy as jnp
from jax import lax
from jax.sharding import PartitionSpec as P

ITERS = 3


damping = 0.2
norm_eps = 1e-05


def silu_slope(preact):
    gating = jax.nn.sigmoid(preact)
    return gating * (1.0 + preact * (1.0 - gating))


def contract_rows(left_side, right_side):
    return lax.dot_general(
        left_side, right_side, (((0,), (0,)), ((), ())), preferred_element_type=jnp.float32
    )


def xor_pairs(size, bit):
    return [(i, i ^ bit) for i in range(size)]


def stages_of(size):
    count = size.bit_length() - 1
    assert 1 << count == size
    return count


def scalar_sum(values, axis):
    names = axis if isinstance(axis, tuple) else (axis,)
    size = 1
    for name in names:
        size *= lax.axis_size(name)
    gathered = lax.all_to_all(jnp.broadcast_to(values[None], (size,) + values.shape), axis, 0, 0)
    return jnp.sum(gathered, axis=0)


def digit_groups(size, widths):
    count = stages_of(size)
    groups, low = [], 0
    for bits in widths:
        if low >= count:
            break
        groups.append((low, min(bits, count - low)))
        low += groups[-1][1]
    if low < count:
        groups.append((low, count - low))
    return groups


def spread_reduce(value, axis, groups, send_type):
    size = lax.axis_size(axis)
    index = lax.axis_index(axis)
    kept = value.astype(jnp.float32)
    for low, bits in groups:
        width = 1 << bits
        digit = (index >> low) & (width - 1)
        rows = kept.shape[0] // width
        total = lax.dynamic_slice_in_dim(kept, digit * rows, rows, 0)
        for offset in range(1, width):
            send = lax.dynamic_slice_in_dim(kept, (digit ^ offset) * rows, rows, 0)
            got = lax.ppermute(send.astype(send_type), axis, xor_pairs(size, offset << low))
            total = total + got.astype(jnp.float32)
        kept = total
    return kept


def spread_gather(chunk, axis, groups):
    size = lax.axis_size(axis)
    index = lax.axis_index(axis)
    for low, bits in reversed(groups):
        width = 1 << bits
        digit = (index >> low) & (width - 1)
        rows = chunk.shape[0]
        whole = jnp.zeros((rows * width,) + chunk.shape[1:], chunk.dtype)
        whole = lax.dynamic_update_slice_in_dim(whole, chunk, digit * rows, 0)
        for offset in range(1, width):
            got = lax.ppermute(chunk, axis, xor_pairs(size, offset << low))
            whole = lax.dynamic_update_slice_in_dim(whole, got, (digit ^ offset) * rows, 0)
        chunk = whole
    return chunk


def fisher_product(direction, residual, normed, hidden_act, slope_act, w_out, w_out_t, metric, width):
    tangent = direction.astype(jnp.bfloat16)
    tangent_in = tangent[:, :width]
    tangent_out_t = tangent[:, width:]
    pre_tangent = jnp.dot(normed, tangent_in, preferred_element_type=jnp.float32)
    inner_tangent = (slope_act * pre_tangent).astype(jnp.bfloat16)
    partial_out = lax.dot_general(
        jnp.concatenate([inner_tangent, hidden_act], axis=1),
        jnp.concatenate([w_out_t, tangent_out_t], axis=1),
        (((1,), (1,)), ((), ())),
        preferred_element_type=jnp.float32,
    )
    fsdp_groups = digit_groups(lax.axis_size("fsdp"), (1, 1, 2))
    out_chunk = spread_reduce(partial_out.astype(jnp.bfloat16), "fsdp", fsdp_groups, jnp.bfloat16)
    cotangent = spread_gather((out_chunk * metric).astype(jnp.bfloat16), "fsdp", fsdp_groups)
    back_act = lax.dot_general(
        cotangent, w_out, (((1,), (1,)), ((), ())), preferred_element_type=jnp.float32
    )
    grad_pre = (slope_act * back_act).astype(jnp.bfloat16)
    part_out_t = contract_rows(cotangent, hidden_act)
    part_in = contract_rows(normed, grad_pre)
    dp_groups = digit_groups(lax.axis_size("dp"), (3,))
    reduced = spread_reduce(jnp.concatenate([part_in, part_out_t], axis=1), "dp", dp_groups, jnp.float32)
    rows = reduced.shape[0]
    start = lax.axis_index("dp") * rows
    direction_chunk = lax.dynamic_slice_in_dim(direction, start, rows, 0)
    residual_chunk = lax.dynamic_slice_in_dim(residual, start, rows, 0)
    fisher_chunk = reduced + damping * direction_chunk
    sums = jnp.stack(
        [
            jnp.sum(direction_chunk * fisher_chunk),
            jnp.sum(residual_chunk * fisher_chunk),
            jnp.sum(fisher_chunk * fisher_chunk),
            jnp.sum(residual_chunk * residual_chunk),
        ]
    )
    fisher = spread_gather(fisher_chunk, "dp", dp_groups)
    return fisher, scalar_sum(sums, ("dp", "fsdp"))


def on_device(states, w_in, w_out, precision, grad_in, grad_out):
    row_count = states.shape[0]
    width = w_in.shape[1]
    metric = precision / (row_count * lax.axis_size("dp"))
    wide_states = states.astype(jnp.float32)
    mean_square = jnp.mean(wide_states * wide_states, axis=1, keepdims=True)
    normed = (wide_states * lax.rsqrt(mean_square + norm_eps)).astype(jnp.bfloat16)
    preact = jnp.dot(normed, w_in, preferred_element_type=jnp.float32)
    hidden_act = jax.nn.silu(preact).astype(jnp.bfloat16)
    slope_act = silu_slope(preact)
    w_out_t = w_out.T
    residual = jnp.concatenate([grad_in, grad_out.T], axis=1)

    def iterate(_, carry):
        solution_now, residual, direction = carry
        fisher, sums = fisher_product(
            direction, residual, normed, hidden_act, slope_act, w_out, w_out_t, metric, width
        )
        quadratic, cross, fisher_square, norm_now = sums
        step_size = norm_now / quadratic
        solution_now = solution_now + step_size * direction
        residual_next = residual - step_size * fisher
        norm_next = norm_now - 2.0 * step_size * cross + step_size * step_size * fisher_square
        direction = residual_next + norm_next / norm_now * direction
        return (solution_now, residual_next, direction)

    solution_now, residual, _ = lax.fori_loop(
        0, ITERS, iterate, (jnp.zeros_like(residual), residual, residual)
    )
    return (
        solution_now[:, :width],
        solution_now[:, width:].T,
        residual[:, :width],
        residual[:, width:].T,
    )


def solution(mesh):
    return jax.shard_map(
        on_device,
        mesh=mesh,
        in_specs=(
            P("dp", None),
            P(None, "fsdp"),
            P("fsdp", None),
            P(),
            P(None, "fsdp"),
            P("fsdp", None),
        ),
        out_specs=(P(None, "fsdp"), P("fsdp", None), P(None, "fsdp"), P("fsdp", None)),
        check_vma=False,
    )
```

```python
import jax
import jax.numpy as jnp
from jax import lax
from jax.sharding import PartitionSpec as P

ITERS = 3


damping = 0.2
norm_eps = 1e-05


def silu_slope(preact):
    gating = jax.nn.sigmoid(preact)
    return gating * (1.0 + preact * (1.0 - gating))


def contract_rows(left_side, right_side):
    return lax.dot_general(
        left_side, right_side, (((0,), (0,)), ((), ())), preferred_element_type=jnp.float32
    )


def xor_pairs(size, bit):
    return [(i, i ^ bit) for i in range(size)]


def stages_of(size):
    count = size.bit_length() - 1
    assert 1 << count == size
    return count


def scalar_sum(values, axis):
    names = axis if isinstance(axis, tuple) else (axis,)
    size = 1
    for name in names:
        size *= lax.axis_size(name)
    gathered = lax.all_to_all(jnp.broadcast_to(values[None], (size,) + values.shape), axis, 0, 0)
    return jnp.sum(gathered, axis=0)


def digit_groups(size, widths):
    count = stages_of(size)
    groups, low = [], 0
    for bits in widths:
        if low >= count:
            break
        groups.append((low, min(bits, count - low)))
        low += groups[-1][1]
    if low < count:
        groups.append((low, count - low))
    return groups


def spread_reduce(value, axis, groups, send_type):
    size = lax.axis_size(axis)
    index = lax.axis_index(axis)
    kept = value.astype(jnp.float32)
    for low, bits in groups:
        width = 1 << bits
        digit = (index >> low) & (width - 1)
        rows = kept.shape[0] // width
        total = lax.dynamic_slice_in_dim(kept, digit * rows, rows, 0)
        for offset in range(1, width):
            send = lax.dynamic_slice_in_dim(kept, (digit ^ offset) * rows, rows, 0)
            got = lax.ppermute(send.astype(send_type), axis, xor_pairs(size, offset << low))
            total = total + got.astype(jnp.float32)
        kept = total
    return kept


def spread_gather(chunk, axis, groups):
    size = lax.axis_size(axis)
    index = lax.axis_index(axis)
    for low, bits in reversed(groups):
        width = 1 << bits
        digit = (index >> low) & (width - 1)
        rows = chunk.shape[0]
        whole = jnp.zeros((rows * width,) + chunk.shape[1:], chunk.dtype)
        whole = lax.dynamic_update_slice_in_dim(whole, chunk, digit * rows, 0)
        for offset in range(1, width):
            got = lax.ppermute(chunk, axis, xor_pairs(size, offset << low))
            whole = lax.dynamic_update_slice_in_dim(whole, got, (digit ^ offset) * rows, 0)
        chunk = whole
    return chunk


def fisher_product(direction, residual, normed, hidden_act, slope_act, w_out, metric, width):
    tangent = direction.astype(jnp.bfloat16)
    tangent_in = tangent[:, :width]
    tangent_out_t = tangent[:, width:]
    pre_tangent = jnp.dot(normed, tangent_in, preferred_element_type=jnp.float32)
    inner_tangent = (slope_act * pre_tangent).astype(jnp.bfloat16)
    partial_out = jnp.dot(inner_tangent, w_out, preferred_element_type=jnp.float32)
    partial_out = partial_out + lax.dot_general(
        hidden_act, tangent_out_t, (((1,), (1,)), ((), ())), preferred_element_type=jnp.float32
    )
    fsdp_groups = digit_groups(lax.axis_size("fsdp"), (1, 1, 1))
    out_chunk = spread_reduce(partial_out.astype(jnp.bfloat16), "fsdp", fsdp_groups, jnp.bfloat16)
    cotangent = spread_gather((out_chunk * metric).astype(jnp.bfloat16), "fsdp", fsdp_groups)
    back_act = lax.dot_general(
        cotangent, w_out, (((1,), (1,)), ((), ())), preferred_element_type=jnp.float32
    )
    grad_pre = (slope_act * back_act).astype(jnp.bfloat16)
    part_out_t = contract_rows(cotangent, hidden_act)
    part_in = contract_rows(normed, grad_pre)
    dp_groups = digit_groups(lax.axis_size("dp"), (3,))
    reduced = spread_reduce(jnp.concatenate([part_in, part_out_t], axis=1), "dp", dp_groups, jnp.float32)
    rows = reduced.shape[0]
    start = lax.axis_index("dp") * rows
    direction_chunk = lax.dynamic_slice_in_dim(direction, start, rows, 0)
    residual_chunk = lax.dynamic_slice_in_dim(residual, start, rows, 0)
    fisher_chunk = reduced + damping * direction_chunk
    sums = jnp.stack(
        [
            jnp.sum(direction_chunk * fisher_chunk),
            jnp.sum(residual_chunk * fisher_chunk),
            jnp.sum(fisher_chunk * fisher_chunk),
            jnp.sum(residual_chunk * residual_chunk),
        ]
    )
    fisher = spread_gather(fisher_chunk, "dp", dp_groups)
    return fisher, scalar_sum(sums, ("dp", "fsdp"))


def on_device(states, w_in, w_out, precision, grad_in, grad_out):
    row_count = states.shape[0]
    width = w_in.shape[1]
    metric = precision / (row_count * lax.axis_size("dp"))
    wide_states = states.astype(jnp.float32)
    mean_square = jnp.mean(wide_states * wide_states, axis=1, keepdims=True)
    normed = (wide_states * lax.rsqrt(mean_square + norm_eps)).astype(jnp.bfloat16)
    preact = jnp.dot(normed, w_in, preferred_element_type=jnp.float32)
    hidden_act = jax.nn.silu(preact).astype(jnp.bfloat16)
    slope_act = silu_slope(preact)
    residual = jnp.concatenate([grad_in, grad_out.T], axis=1)

    def iterate(_, carry):
        solution_now, residual, direction = carry
        fisher, sums = fisher_product(
            direction, residual, normed, hidden_act, slope_act, w_out, metric, width
        )
        quadratic, cross, fisher_square, norm_now = sums
        step_size = norm_now / quadratic
        solution_now = solution_now + step_size * direction
        residual_next = residual - step_size * fisher
        norm_next = norm_now - 2.0 * step_size * cross + step_size * step_size * fisher_square
        direction = residual_next + norm_next / norm_now * direction
        return (solution_now, residual_next, direction)

    solution_now, residual, _ = lax.fori_loop(
        0, ITERS, iterate, (jnp.zeros_like(residual), residual, residual)
    )
    return (
        solution_now[:, :width],
        solution_now[:, width:].T,
        residual[:, :width],
        residual[:, width:].T,
    )


def solution(mesh):
    return jax.shard_map(
        on_device,
        mesh=mesh,
        in_specs=(
            P("dp", None),
            P(None, "fsdp"),
            P("fsdp", None),
            P(),
            P(None, "fsdp"),
            P("fsdp", None),
        ),
        out_specs=(P(None, "fsdp"), P("fsdp", None), P(None, "fsdp"), P("fsdp", None)),
        check_vma=False,
    )
```

```python
import jax
import jax.numpy as jnp
from jax import lax
from jax.sharding import PartitionSpec as P

ITERS = 3


damping = 0.2
norm_eps = 1e-05


def silu_slope(preact):
    gating = jax.nn.sigmoid(preact)
    return gating * (1.0 + preact * (1.0 - gating))


def contract_rows(left_side, right_side):
    return lax.dot_general(
        left_side, right_side, (((0,), (0,)), ((), ())), preferred_element_type=jnp.float32
    )


def xor_pairs(size, bit):
    return [(i, i ^ bit) for i in range(size)]


def stages_of(size):
    count = size.bit_length() - 1
    assert 1 << count == size
    return count


def scalar_sum(values, axis):
    names = axis if isinstance(axis, tuple) else (axis,)
    size = 1
    for name in names:
        size *= lax.axis_size(name)
    gathered = lax.all_to_all(jnp.broadcast_to(values[None], (size,) + values.shape), axis, 0, 0)
    return jnp.sum(gathered, axis=0)


def digit_groups(size, widths):
    count = stages_of(size)
    groups, low = [], 0
    for bits in widths:
        if low >= count:
            break
        groups.append((low, min(bits, count - low)))
        low += groups[-1][1]
    if low < count:
        groups.append((low, count - low))
    return groups


def spread_reduce(value, axis, groups, send_type):
    size = lax.axis_size(axis)
    index = lax.axis_index(axis)
    kept = value.astype(jnp.float32)
    for low, bits in groups:
        width = 1 << bits
        digit = (index >> low) & (width - 1)
        rows = kept.shape[0] // width
        total = lax.dynamic_slice_in_dim(kept, digit * rows, rows, 0)
        for offset in range(1, width):
            send = lax.dynamic_slice_in_dim(kept, (digit ^ offset) * rows, rows, 0)
            got = lax.ppermute(send.astype(send_type), axis, xor_pairs(size, offset << low))
            total = total + got.astype(jnp.float32)
        kept = total
    return kept


def spread_gather(chunk, axis, groups):
    size = lax.axis_size(axis)
    index = lax.axis_index(axis)
    for low, bits in reversed(groups):
        width = 1 << bits
        digit = (index >> low) & (width - 1)
        rows = chunk.shape[0]
        whole = jnp.zeros((rows * width,) + chunk.shape[1:], chunk.dtype)
        whole = lax.dynamic_update_slice_in_dim(whole, chunk, digit * rows, 0)
        for offset in range(1, width):
            got = lax.ppermute(chunk, axis, xor_pairs(size, offset << low))
            whole = lax.dynamic_update_slice_in_dim(whole, got, (digit ^ offset) * rows, 0)
        chunk = whole
    return chunk


def fisher_product(direction, residual, normed, hidden_act, slope_act, w_out, metric, width):
    tangent = direction.astype(jnp.bfloat16)
    tangent_in = tangent[:, :width]
    tangent_out_t = tangent[:, width:]
    pre_tangent = jnp.dot(normed, tangent_in, preferred_element_type=jnp.float32)
    inner_tangent = (slope_act * pre_tangent).astype(jnp.bfloat16)
    partial_out = jnp.dot(inner_tangent, w_out, preferred_element_type=jnp.float32)
    partial_out = partial_out + lax.dot_general(
        hidden_act, tangent_out_t, (((1,), (1,)), ((), ())), preferred_element_type=jnp.float32
    )
    fsdp_groups = digit_groups(lax.axis_size("fsdp"), (1, 1, 1, 1))
    out_chunk = spread_reduce(partial_out.astype(jnp.bfloat16), "fsdp", fsdp_groups, jnp.bfloat16)
    cotangent = spread_gather((out_chunk * metric).astype(jnp.bfloat16), "fsdp", fsdp_groups)
    back_act = lax.dot_general(
        cotangent, w_out, (((1,), (1,)), ((), ())), preferred_element_type=jnp.float32
    )
    grad_pre = (slope_act * back_act).astype(jnp.bfloat16)
    part_out_t = contract_rows(cotangent, hidden_act)
    part_in = contract_rows(normed, grad_pre)
    dp_groups = digit_groups(lax.axis_size("dp"), (3,))
    reduced = spread_reduce(jnp.concatenate([part_in, part_out_t], axis=1), "dp", dp_groups, jnp.float32)
    rows = reduced.shape[0]
    start = lax.axis_index("dp") * rows
    direction_chunk = lax.dynamic_slice_in_dim(direction, start, rows, 0)
    residual_chunk = lax.dynamic_slice_in_dim(residual, start, rows, 0)
    fisher_chunk = reduced + damping * direction_chunk
    sums = jnp.stack(
        [
            jnp.sum(direction_chunk * fisher_chunk),
            jnp.sum(residual_chunk * fisher_chunk),
            jnp.sum(fisher_chunk * fisher_chunk),
            jnp.sum(residual_chunk * residual_chunk),
        ]
    )
    fisher = spread_gather(fisher_chunk, "dp", dp_groups)
    return fisher, scalar_sum(sums, ("dp", "fsdp"))


def on_device(states, w_in, w_out, precision, grad_in, grad_out):
    row_count = states.shape[0]
    width = w_in.shape[1]
    metric = precision / (row_count * lax.axis_size("dp"))
    wide_states = states.astype(jnp.float32)
    mean_square = jnp.mean(wide_states * wide_states, axis=1, keepdims=True)
    normed = (wide_states * lax.rsqrt(mean_square + norm_eps)).astype(jnp.bfloat16)
    preact = jnp.dot(normed, w_in, preferred_element_type=jnp.float32)
    hidden_act = jax.nn.silu(preact).astype(jnp.bfloat16)
    slope_act = silu_slope(preact)
    residual = jnp.concatenate([grad_in, grad_out.T], axis=1)

    def iterate(_, carry):
        solution_now, residual, direction = carry
        fisher, sums = fisher_product(
            direction, residual, normed, hidden_act, slope_act, w_out, metric, width
        )
        quadratic, cross, fisher_square, norm_now = sums
        step_size = norm_now / quadratic
        solution_now = solution_now + step_size * direction
        residual_next = residual - step_size * fisher
        norm_next = norm_now - 2.0 * step_size * cross + step_size * step_size * fisher_square
        direction = residual_next + norm_next / norm_now * direction
        return (solution_now, residual_next, direction)

    solution_now, residual, _ = lax.fori_loop(
        0, ITERS, iterate, (jnp.zeros_like(residual), residual, residual)
    )
    return (
        solution_now[:, :width],
        solution_now[:, width:].T,
        residual[:, :width],
        residual[:, width:].T,
    )


def solution(mesh):
    return jax.shard_map(
        on_device,
        mesh=mesh,
        in_specs=(
            P("dp", None),
            P(None, "fsdp"),
            P("fsdp", None),
            P(),
            P(None, "fsdp"),
            P("fsdp", None),
        ),
        out_specs=(P(None, "fsdp"), P("fsdp", None), P(None, "fsdp"), P("fsdp", None)),
        check_vma=False,
    )
```
